512 devices in a mesh: row: 32 (over z, x), col: 16 (over y, core).
Axes of the slice: x: 4, y: 8, z: 8, core: 2. Of those that a mesh axis runs over, the one named last changes fastest.
Arguments:
- coeffs: float32 [4096, 128], P(('row', 'col')), may hold values from -6 to 6
- basis: float32 [256, 128, 4096], P('row', 'col'), may hold values from -0.1875 to 0.1875
- observed: float32 [256, 128, 128], P('row', 'col'), may hold values from -6 to 6
- lift_w: float32 [32], replicated, may hold values from -3 to 3
- lift_b: float32 [32], replicated, may hold values from -3 to 3
- w_one: bfloat16 [3, 3, 32, 32], replicated, may hold values from -0.375 to 0.375
- b_one: float32 [32], replicated, may hold values from -3 to 3
- w_two: bfloat16 [3, 3, 32, 32], replicated, may hold values from -0.375 to 0.375
- b_two: float32 [32], replicated, may hold values from -3 to 3
- read_w: float32 [32], replicated, may hold values from -1 to 1
Outputs:
- pressure: float32 [256, 128, 128], P('row', 'col')
- grad_coeffs: float32 [4096, 128], P(('row', 'col'))
The draws below stay inside these ranges and needn't reach their ends.
All inputs are finite; a program needn't handle non-finite values.
Results may differ from the reference program's by a relative error of at most 0.015.
Values may be sent and summed in bfloat16 or wider, within the bound.
No kernel may reach another device: no remote copies, remote signals or barrier semaphores. Data moves between devices by JAX's collectives and lax.ppermute only.
A program may use at most 64 MiB of HBM per device.

```python
import math
import jax
import jax.numpy as jnp
from jax import lax

M = 4096
C = 32
B = 128
NX = 256
NY = 128


def with_spikes(drawn, rng, source, target, blocks, factor):
    owner, partner = [(jnp.arange(drawn.shape[axis_at]) // (drawn.shape[axis_at] // blocks)).reshape([-1 if axis == axis_at else 1 for axis in range(drawn.ndim)]) for axis_at in (source, target)]
    chosen = jax.random.permutation(rng, blocks)[partner]
    strong = (owner == chosen) | (owner == (partner + blocks // 2) % blocks)
    return jnp.where(strong, factor * drawn, drawn)


def shard_levels(stream_key, extent, split, smallest, high):
    gain, own = 1.0, jax.random.fold_in(stream_key, 6)
    for dim, parts in split:
        heights = jnp.exp(jax.random.uniform(jax.random.fold_in(own, dim), (parts,), jnp.float32, smallest / len(split), high / len(split)))
        gain = gain * jnp.repeat(heights, extent[dim] // parts).reshape([-1 if axis == dim else 1 for axis in range(len(extent))])
    return gain


def noise(own_key, shape, deviation, most, shards=(), kind=jnp.bfloat16):
    entries = jax.random.normal(own_key, shape, jnp.float32) * deviation
    if len(shards) > 0:
        entries = shard_levels(own_key, shape, shards, -0.22, 0.18) * entries
    return jnp.clip(entries, min=-most, max=most).astype(kind)


def gaussian_with(key, dims, width, reach, shards, heavy, kind=jnp.bfloat16):
    entries = width * jax.random.normal(key, dims, jnp.float32)
    if shards:
        entries = entries * shard_levels(key, dims, shards, -0.22, 0.18)
    return jnp.clip(with_spikes(entries, jax.random.fold_in(key, 3), *heavy), -reach, reach).astype(kind)


def setup_inputs(seed: int = 0) -> dict:
    arg_keys = jax.random.split(jax.random.key(seed), 11)
    coeffs = noise(arg_keys[0], (M, B), 1.0, 6.0, ((0, 512),), jnp.float32)
    basis = gaussian_with(arg_keys[1], (NX, NY, M), M ** -0.5, 0.1875, ((0, 32), (1, 16)), (0, 2, 32, 2.75), jnp.float32)
    observed = noise(arg_keys[2], (NX, NY, B), 1.0, 6.0, ((0, 32), (1, 16)), jnp.float32)
    lift_w = noise(arg_keys[3], (C,), 1.0, 3.0, (), jnp.float32)
    lift_b = noise(arg_keys[4], (C,), 0.5, 3.0, (), jnp.float32)
    w_one = noise(arg_keys[5], (3, 3, C, C), (9 * C) ** -0.5, 0.375)
    b_one = noise(arg_keys[6], (C,), 0.3, 3.0, (), jnp.float32)
    w_two = noise(arg_keys[7], (3, 3, C, C), (9 * C) ** -0.5, 0.375)
    b_two = noise(arg_keys[8], (C,), 0.3, 3.0, (), jnp.float32)
    read_w = noise(arg_keys[9], (C,), C ** -0.5, 1.0, (), jnp.float32)
    return {"coeffs": coeffs, "basis": basis, "observed": observed, "lift_w": lift_w, "lift_b": lift_b, "w_one": w_one, "b_one": b_one, "w_two": w_two, "b_two": b_two, "read_w": read_w}


prior_weight = 0.1


def conv_fwd(values, weights):
    padded = jnp.pad(values.astype(jnp.float32), ((1, 1), (1, 1), (0, 0), (0, 0)))
    nrow = values.shape[0]
    ncol = values.shape[1]
    running = jnp.zeros(values.shape[:3] + (weights.shape[3],), jnp.float32)
    for shift_x in range(3):
        for shift_y in range(3):
            window = padded[shift_x:shift_x + nrow, shift_y:shift_y + ncol]
            running = running + jnp.einsum("xybi,io->xybo", window, weights[shift_x, shift_y].astype(jnp.float32))
    return running


def conv_back(grads, weights):
    padded = jnp.pad(grads.astype(jnp.float32), ((1, 1), (1, 1), (0, 0), (0, 0)))
    nrow = grads.shape[0]
    ncol = grads.shape[1]
    running = jnp.zeros(grads.shape[:3] + (weights.shape[2],), jnp.float32)
    for shift_x in range(3):
        for shift_y in range(3):
            window = padded[2 - shift_x:2 - shift_x + nrow, 2 - shift_y:2 - shift_y + ncol]
            running = running + jnp.einsum("xybo,io->xybi", window, weights[shift_x, shift_y].astype(jnp.float32))
    return running


def reference(coeffs, basis, observed, lift_w, lift_b, w_one, b_one, w_two, b_two, read_w):
    flat_basis = basis.reshape(NX * NY, M)
    logperm = jnp.dot(flat_basis, coeffs, precision=lax.Precision.HIGHEST, preferred_element_type=jnp.float32)
    block_size = math.gcd(B, 8)
    nblocks = B // block_size
    field_blocks = jnp.moveaxis(logperm.reshape(NX, NY, nblocks, block_size), 2, 0)
    obs_blocks = jnp.moveaxis(observed.reshape(NX, NY, nblocks, block_size), 2, 0)

    def surrogate(pair):
        field_vals, obs_vals = pair
        lifted = (field_vals[..., None] * lift_w + lift_b).astype(jnp.bfloat16)
        hidden_one = jnp.tanh(conv_fwd(lifted, w_one) + b_one).astype(jnp.bfloat16)
        hidden_two = jnp.tanh(conv_fwd(hidden_one, w_two) + b_two)
        press = jnp.sum(hidden_two * read_w, axis=-1)
        misfit = press - obs_vals
        grad_two = (misfit[..., None] * read_w * (1.0 - hidden_two * hidden_two)).astype(jnp.bfloat16)
        h_one = hidden_one.astype(jnp.float32)
        grad_one = (conv_back(grad_two, w_two) * (1.0 - h_one * h_one)).astype(jnp.bfloat16)
        grad_field = jnp.sum(conv_back(grad_one, w_one) * lift_w, axis=-1)
        return press, grad_field

    press_blocks, grad_blocks = lax.map(surrogate, (field_blocks, obs_blocks))
    pressure = jnp.moveaxis(press_blocks, 0, 2).reshape(NX, NY, B)
    grad_field = jnp.moveaxis(grad_blocks, 0, 2).reshape(NX * NY, B)
    grad_coeffs = jnp.dot(flat_basis.T, grad_field, precision=lax.Precision.HIGHEST, preferred_element_type=jnp.float32) + prior_weight * coeffs
    return pressure, grad_coeffs
```

```python
import jax
import jax.numpy as jnp
from jax import lax
from jax.sharding import Mesh, PartitionSpec as P
import numpy as np

prior_weight = 0.1


ROW_AXES = ("z", "x")
COL_AXES = ("y", "core")
ALL_AXES = ROW_AXES + COL_AXES


def with_halo(block, sides, width):
    for axis, dim in sides:
        count = lax.axis_size(axis)
        forward = [(i, i + 1) for i in range(count - 1)]
        backward = [(target, source) for source, target in forward]
        low = lax.ppermute(
            lax.slice_in_dim(block, block.shape[dim] - width, None, axis=dim), axis, forward
        )
        high = lax.ppermute(lax.slice_in_dim(block, 0, width, axis=dim), axis, backward)
        block = jnp.concatenate([low, block, high], axis=dim)
    return block


def extend_tile(values):
    return with_halo(values, ((ROW_AXES, 0), (COL_AXES, 1)), 1)


def conv_fwd(values, weights, extend):
    padded = extend(values)
    nrow = values.shape[0]
    ncol = values.shape[1]
    running = jnp.zeros(values.shape[:3] + (weights.shape[3],), jnp.float32)
    for shift_x in range(3):
        for shift_y in range(3):
            window = padded[shift_x : shift_x + nrow, shift_y : shift_y + ncol]
            running = running + jnp.einsum(
                "xybi,io->xybo",
                window,
                weights[shift_x, shift_y],
                preferred_element_type=jnp.float32,
            )
    return running


def conv_back(grads, weights, extend):
    padded = extend(grads)
    nrow = grads.shape[0]
    ncol = grads.shape[1]
    running = jnp.zeros(grads.shape[:3] + (weights.shape[2],), jnp.float32)
    for shift_x in range(3):
        for shift_y in range(3):
            window = padded[2 - shift_x : 2 - shift_x + nrow, 2 - shift_y : 2 - shift_y + ncol]
            running = running + jnp.einsum(
                "xybo,io->xybi",
                window,
                weights[shift_x, shift_y],
                preferred_element_type=jnp.float32,
            )
    return running


def surrogate(logperm, observed, lift_w, lift_b, w_one, b_one, w_two, b_two, read_w, extend):
    lifted = (logperm[..., None] * lift_w + lift_b).astype(jnp.bfloat16)
    hidden_one = jnp.tanh(conv_fwd(lifted, w_one, extend) + b_one).astype(jnp.bfloat16)
    hidden_two = jnp.tanh(conv_fwd(hidden_one, w_two, extend) + b_two)
    pressure = jnp.sum(hidden_two * read_w, axis=-1)
    misfit = pressure - observed
    grad_two = (misfit[..., None] * read_w * (1.0 - hidden_two * hidden_two)).astype(jnp.bfloat16)
    h_one = hidden_one.astype(jnp.float32)
    grad_one = (conv_back(grad_two, w_two, extend) * (1.0 - h_one * h_one)).astype(jnp.bfloat16)
    grad_field = jnp.sum(conv_back(grad_one, w_one, extend) * lift_w, axis=-1)
    return (pressure, grad_field)


def shards(coeffs, basis, observed, lift_w, lift_b, w_one, b_one, w_two, b_two, read_w):
    tile_rows, tile_cols, mode_count = basis.shape
    batch_size = coeffs.shape[1]
    flat_basis = basis.reshape(tile_rows * tile_cols, mode_count)
    basis_part = flat_basis
    gathered = coeffs
    for position, axis in enumerate(ALL_AXES):
        gathered = lax.all_gather(gathered, axis, axis=position, tiled=False)
    gathered = gathered.reshape(-1, batch_size)
    logperm = jnp.dot(
        basis_part,
        gathered,
        precision=lax.Precision.HIGHEST,
        preferred_element_type=jnp.float32,
    )
    logperm = logperm.reshape(tile_rows, tile_cols, batch_size)
    pressure, grad_field = surrogate(
        logperm, observed, lift_w, lift_b, w_one, b_one, w_two, b_two, read_w, extend_tile
    )
    grad_flat = grad_field.reshape(tile_rows * tile_cols, batch_size)
    basis_part = flat_basis
    projected = lax.dot_general(
        basis_part,
        grad_flat,
        (((0,), (0,)), ((), ())),
        precision=lax.Precision.HIGHEST,
        preferred_element_type=jnp.float32,
    )
    sizes = tuple(lax.axis_size(axis) for axis in ALL_AXES)
    summed = projected.reshape(sizes + (coeffs.shape[0], batch_size))
    for position in reversed(range(len(ALL_AXES))):
        summed = lax.psum_scatter(summed, ALL_AXES[position], scatter_dimension=position, tiled=False)
    grad_coeffs = summed + prior_weight * coeffs
    return (pressure, grad_coeffs)


def solution(mesh):
    row_size, col_size = mesh.devices.shape
    fine = Mesh(mesh.devices.reshape(row_size // 8, 8, col_size // 2, 2), ALL_AXES)
    return jax.shard_map(
        shards,
        mesh=fine,
        in_specs=(
            P(ALL_AXES, None),
            P(ROW_AXES, COL_AXES, None),
            P(ROW_AXES, COL_AXES, None),
            P(),
            P(),
            P(),
            P(),
            P(),
            P(),
            P(),
        ),
        out_specs=(P(ROW_AXES, COL_AXES, None), P(ALL_AXES, None)),
        check_vma=False,
    )
```

```python
import jax
import jax.numpy as jnp
from jax import lax
from jax.sharding import Mesh, PartitionSpec as P
import numpy as np

prior_weight = 0.1


ROW_AXES = ("z", "x")
COL_AXES = ("y", "core")
ALL_AXES = ROW_AXES + COL_AXES


def with_halo(block, sides, width):
    for axis, dim in sides:
        count = lax.axis_size(axis)
        forward = [(i, i + 1) for i in range(count - 1)]
        backward = [(target, source) for source, target in forward]
        low = lax.ppermute(
            lax.slice_in_dim(block, block.shape[dim] - width, None, axis=dim), axis, forward
        )
        high = lax.ppermute(lax.slice_in_dim(block, 0, width, axis=dim), axis, backward)
        block = jnp.concatenate([low, block, high], axis=dim)
    return block


def extend_tile(values):
    return with_halo(values, ((ROW_AXES, 0), (COL_AXES, 1)), 1)


def conv_fwd(values, weights, extend):
    padded = extend(values)
    nrow = values.shape[0]
    ncol = values.shape[1]
    running = jnp.zeros(values.shape[:3] + (weights.shape[3],), jnp.float32)
    for shift_x in range(3):
        for shift_y in range(3):
            window = padded[shift_x : shift_x + nrow, shift_y : shift_y + ncol]
            running = running + jnp.einsum(
                "xybi,io->xybo",
                window,
                weights[shift_x, shift_y],
                preferred_element_type=jnp.float32,
            )
    return running


def conv_back(grads, weights, extend):
    padded = extend(grads)
    nrow = grads.shape[0]
    ncol = grads.shape[1]
    running = jnp.zeros(grads.shape[:3] + (weights.shape[2],), jnp.float32)
    for shift_x in range(3):
        for shift_y in range(3):
            window = padded[2 - shift_x : 2 - shift_x + nrow, 2 - shift_y : 2 - shift_y + ncol]
            running = running + jnp.einsum(
                "xybo,io->xybi",
                window,
                weights[shift_x, shift_y],
                preferred_element_type=jnp.float32,
            )
    return running


def surrogate(logperm, observed, lift_w, lift_b, w_one, b_one, w_two, b_two, read_w, extend):
    lifted = (logperm[..., None] * lift_w + lift_b).astype(jnp.bfloat16)
    hidden_one = jnp.tanh(conv_fwd(lifted, w_one, extend) + b_one).astype(jnp.bfloat16)
    hidden_two = jnp.tanh(conv_fwd(hidden_one, w_two, extend) + b_two)
    pressure = jnp.sum(hidden_two * read_w, axis=-1)
    misfit = pressure - observed
    grad_two = (misfit[..., None] * read_w * (1.0 - hidden_two * hidden_two)).astype(jnp.bfloat16)
    h_one = hidden_one.astype(jnp.float32)
    grad_one = (conv_back(grad_two, w_two, extend) * (1.0 - h_one * h_one)).astype(jnp.bfloat16)
    grad_field = jnp.sum(conv_back(grad_one, w_one, extend) * lift_w, axis=-1)
    return (pressure, grad_field)


def bit_order(sizes):
    groups = []
    low = 0
    for size in reversed(sizes):
        width = size.bit_length() - 1
        groups.append(list(range(low, low + width)))
        low += width
    core_bits, rest = groups[0], groups[1:]
    order = list(core_bits)
    depth = 0
    while any(depth < len(group) for group in rest):
        for group in rest:
            if depth < len(group):
                order.append(group[depth])
        depth += 1
    return order, low


def exchange(values, bit, count):
    pairs = [(i, i ^ (1 << bit)) for i in range(count)]
    return lax.ppermute(values, ALL_AXES, pairs)


def scatter_sum(projected, mode_block, sizes):
    order, nbits = bit_order(sizes)
    count = 1 << nbits
    me = lax.axis_index(ALL_AXES)
    data = projected.reshape((2,) * nbits + (mode_block, projected.shape[1]))
    present = list(range(nbits - 1, -1, -1))
    for bit in order:
        dim = present.index(bit)
        mine = (me >> bit) & 1
        keep = lax.dynamic_index_in_dim(data, mine, axis=dim, keepdims=False)
        send = lax.dynamic_index_in_dim(data, 1 - mine, axis=dim, keepdims=False)
        data = keep + exchange(send, bit, count)
        present.pop(dim)
    return data


def gather_all(block, sizes):
    order, nbits = bit_order(sizes)
    count = 1 << nbits
    me = lax.axis_index(ALL_AXES)
    data = block
    present = []
    for bit in reversed(order):
        mine = (me >> bit) & 1
        other = exchange(data, bit, count)
        low = jnp.where(mine == 0, data, other)
        high = jnp.where(mine == 0, other, data)
        dim = sum(1 for b in present if b > bit)
        data = jnp.stack([low, high], axis=dim)
        present.insert(dim, bit)
    return data.reshape(count * block.shape[0], block.shape[1])


def shards(coeffs, basis, observed, lift_w, lift_b, w_one, b_one, w_two, b_two, read_w):
    tile_rows, tile_cols, mode_count = basis.shape
    batch_size = coeffs.shape[1]
    sizes = tuple(lax.axis_size(axis) for axis in ALL_AXES)
    flat_basis = basis.reshape(tile_rows * tile_cols, mode_count)
    logperm = jnp.dot(
        flat_basis,
        gather_all(coeffs, sizes),
        precision=lax.Precision.HIGHEST,
        preferred_element_type=jnp.float32,
    )
    logperm = logperm.reshape(tile_rows, tile_cols, batch_size)
    pressure, grad_field = surrogate(
        logperm, observed, lift_w, lift_b, w_one, b_one, w_two, b_two, read_w, extend_tile
    )
    grad_flat = grad_field.reshape(tile_rows * tile_cols, batch_size)
    projected = lax.dot_general(
        flat_basis,
        grad_flat,
        (((0,), (0,)), ((), ())),
        precision=lax.Precision.HIGHEST,
        preferred_element_type=jnp.float32,
    )
    summed = scatter_sum(projected, coeffs.shape[0], sizes)
    grad_coeffs = summed + prior_weight * coeffs
    return (pressure, grad_coeffs)


def solution(mesh):
    row_size, col_size = mesh.devices.shape
    fine = Mesh(mesh.devices.reshape(row_size // 8, 8, col_size // 2, 2), ALL_AXES)
    return jax.shard_map(
        shards,
        mesh=fine,
        in_specs=(
            P(ALL_AXES, None),
            P(ROW_AXES, COL_AXES, None),
            P(ROW_AXES, COL_AXES, None),
            P(),
            P(),
            P(),
            P(),
            P(),
            P(),
            P(),
        ),
        out_specs=(P(ROW_AXES, COL_AXES, None), P(ALL_AXES, None)),
        check_vma=False,
    )
```

```python
import jax
import jax.numpy as jnp
from jax import lax
from jax.sharding import Mesh, PartitionSpec as P
import numpy as np

prior_weight = 0.1


ALL_AXES = tuple(f"b{bit}" for bit in range(8, -1, -1))
ROW_AXES = ALL_AXES[:5]
COL_AXES = ALL_AXES[5:]
FAR_COUNT = 5


def with_halo(block, sides, width):
    for axis, dim in sides:
        count = lax.axis_size(axis)
        forward = [(i, i + 1) for i in range(count - 1)]
        backward = [(target, source) for source, target in forward]
        low = lax.ppermute(
            lax.slice_in_dim(block, block.shape[dim] - width, None, axis=dim), axis, forward
        )
        high = lax.ppermute(lax.slice_in_dim(block, 0, width, axis=dim), axis, backward)
        block = jnp.concatenate([low, block, high], axis=dim)
    return block


def extend_tile(values):
    return with_halo(values, ((ROW_AXES, 0), (COL_AXES, 1)), 1)


def conv_fwd(values, weights, extend):
    padded = extend(values)
    nrow = values.shape[0]
    ncol = values.shape[1]
    running = jnp.zeros(values.shape[:3] + (weights.shape[3],), jnp.float32)
    for shift_x in range(3):
        for shift_y in range(3):
            window = padded[shift_x : shift_x + nrow, shift_y : shift_y + ncol]
            running = running + jnp.einsum(
                "xybi,io->xybo",
                window,
                weights[shift_x, shift_y],
                preferred_element_type=jnp.float32,
            )
    return running


def conv_back(grads, weights, extend):
    padded = extend(grads)
    nrow = grads.shape[0]
    ncol = grads.shape[1]
    running = jnp.zeros(grads.shape[:3] + (weights.shape[2],), jnp.float32)
    for shift_x in range(3):
        for shift_y in range(3):
            window = padded[2 - shift_x : 2 - shift_x + nrow, 2 - shift_y : 2 - shift_y + ncol]
            running = running + jnp.einsum(
                "xybo,io->xybi",
                window,
                weights[shift_x, shift_y],
                preferred_element_type=jnp.float32,
            )
    return running


def surrogate(logperm, observed, lift_w, lift_b, w_one, b_one, w_two, b_two, read_w, extend):
    lifted = (logperm[..., None] * lift_w + lift_b).astype(jnp.bfloat16)
    hidden_one = jnp.tanh(conv_fwd(lifted, w_one, extend) + b_one).astype(jnp.bfloat16)
    hidden_two = jnp.tanh(conv_fwd(hidden_one, w_two, extend) + b_two)
    pressure = jnp.sum(hidden_two * read_w, axis=-1)
    misfit = pressure - observed
    grad_two = (misfit[..., None] * read_w * (1.0 - hidden_two * hidden_two)).astype(jnp.bfloat16)
    h_one = hidden_one.astype(jnp.float32)
    grad_one = (conv_back(grad_two, w_two, extend) * (1.0 - h_one * h_one)).astype(jnp.bfloat16)
    grad_field = jnp.sum(conv_back(grad_one, w_one, extend) * lift_w, axis=-1)
    return (pressure, grad_field)


def bit_order(sizes):
    groups = []
    low = 0
    for size in reversed(sizes):
        width = size.bit_length() - 1
        groups.append(list(range(low, low + width)))
        low += width
    core_bits, rest = groups[0], groups[1:]
    order = list(core_bits)
    depth = 0
    while any(depth < len(group) for group in rest):
        for group in rest:
            if depth < len(group):
                order.append(group[depth])
        depth += 1
    return order, low


def exchange(values, bit, count):
    pairs = [(i, i ^ (1 << bit)) for i in range(count)]
    return lax.ppermute(values, ALL_AXES, pairs)


def scatter_sum(projected, mode_block, sizes):
    order, nbits = bit_order(sizes)
    count = 1 << nbits
    me = lax.axis_index(ALL_AXES)
    data = projected.reshape((2,) * nbits + (mode_block, projected.shape[1]))
    present = list(range(nbits - 1, -1, -1))
    near, far = order[: nbits - FAR_COUNT], order[nbits - FAR_COUNT :]
    for bit in near:
        dim = present.index(bit)
        mine = (me >> bit) & 1
        keep = lax.dynamic_index_in_dim(data, mine, axis=dim, keepdims=False)
        send = lax.dynamic_index_in_dim(data, 1 - mine, axis=dim, keepdims=False)
        data = keep + exchange(send, bit, count)
        present.pop(dim)
    group = tuple(f"b{bit}" for bit in present)
    data = data.reshape((1 << len(present), mode_block, projected.shape[1]))
    data = lax.all_to_all(data, group, 0, 0, tiled=False)
    return jnp.sum(data, axis=0)


def gather_all(block, sizes):
    order, nbits = bit_order(sizes)
    count = 1 << nbits
    me = lax.axis_index(ALL_AXES)
    near, far = order[: nbits - FAR_COUNT], order[nbits - FAR_COUNT :]
    present = sorted(far, reverse=True)
    group = tuple(f"b{bit}" for bit in present)
    data = jnp.broadcast_to(block[None], (1 << len(present),) + block.shape)
    data = lax.all_to_all(data, group, 0, 0, tiled=False)
    data = data.reshape((2,) * len(present) + block.shape)
    for bit in reversed(near):
        mine = (me >> bit) & 1
        other = exchange(data, bit, count)
        low = jnp.where(mine == 0, data, other)
        high = jnp.where(mine == 0, other, data)
        dim = sum(1 for b in present if b > bit)
        data = jnp.stack([low, high], axis=dim)
        present.insert(dim, bit)
    return data.reshape(count * block.shape[0], block.shape[1])


def shards(coeffs, basis, observed, lift_w, lift_b, w_one, b_one, w_two, b_two, read_w):
    tile_rows, tile_cols, mode_count = basis.shape
    batch_size = coeffs.shape[1]
    sizes = (4, 8, 8, 2)
    flat_basis = basis.reshape(tile_rows * tile_cols, mode_count)
    logperm = jnp.dot(
        flat_basis,
        gather_all(coeffs, sizes),
        precision=lax.Precision.HIGHEST,
        preferred_element_type=jnp.float32,
    )
    logperm = logperm.reshape(tile_rows, tile_cols, batch_size)
    pressure, grad_field = surrogate(
        logperm, observed, lift_w, lift_b, w_one, b_one, w_two, b_two, read_w, extend_tile
    )
    grad_flat = grad_field.reshape(tile_rows * tile_cols, batch_size)
    projected = lax.dot_general(
        flat_basis,
        grad_flat,
        (((0,), (0,)), ((), ())),
        precision=lax.Precision.HIGHEST,
        preferred_element_type=jnp.float32,
    )
    summed = scatter_sum(projected, coeffs.shape[0], sizes)
    grad_coeffs = summed + prior_weight * coeffs
    return (pressure, grad_coeffs)


def solution(mesh):
    row_size, col_size = mesh.devices.shape
    fine = Mesh(mesh.devices.reshape((2,) * len(ALL_AXES)), ALL_AXES)
    return jax.shard_map(
        shards,
        mesh=fine,
        in_specs=(
            P(ALL_AXES, None),
            P(ROW_AXES, COL_AXES, None),
            P(ROW_AXES, COL_AXES, None),
            P(),
            P(),
            P(),
            P(),
            P(),
            P(),
            P(),
        ),
        out_specs=(P(ROW_AXES, COL_AXES, None), P(ALL_AXES, None)),
        check_vma=False,
    )
```

```python
import jax
import jax.numpy as jnp
from jax import lax
from jax.sharding import Mesh, PartitionSpec as P
import numpy as np

prior_weight = 0.1


ALL_AXES = tuple(f"b{bit}" for bit in range(8, -1, -1))
ROW_AXES = ALL_AXES[:5]
COL_AXES = ALL_AXES[5:]
FAR_COUNT = 5


def with_halo(block, sides, width):
    for axis, dim in sides:
        count = lax.axis_size(axis)
        forward = [(i, i + 1) for i in range(count - 1)]
        backward = [(target, source) for source, target in forward]
        low = lax.ppermute(
            lax.slice_in_dim(block, block.shape[dim] - width, None, axis=dim), axis, forward
        )
        high = lax.ppermute(lax.slice_in_dim(block, 0, width, axis=dim), axis, backward)
        block = jnp.concatenate([low, block, high], axis=dim)
    return block


HALO = 4


def inside_grid(tile_rows, tile_cols, halo):
    row_count = lax.axis_size(ROW_AXES)
    col_count = lax.axis_size(COL_AXES)
    rows = lax.axis_index(ROW_AXES) * tile_rows - halo + jnp.arange(tile_rows + 2 * halo)
    cols = lax.axis_index(COL_AXES) * tile_cols - halo + jnp.arange(tile_cols + 2 * halo)
    row_ok = (rows >= 0) & (rows < row_count * tile_rows)
    col_ok = (cols >= 0) & (cols < col_count * tile_cols)
    return (row_ok[:, None] & col_ok[None, :])[:, :, None, None]


def conv_valid(values, weights):
    nrow = values.shape[0] - 2
    ncol = values.shape[1] - 2
    running = jnp.zeros((nrow, ncol) + values.shape[2:3] + (weights.shape[3],), jnp.float32)
    for shift_x in range(3):
        for shift_y in range(3):
            window = values[shift_x : shift_x + nrow, shift_y : shift_y + ncol]
            running = running + jnp.einsum(
                "xybi,io->xybo",
                window,
                weights[shift_x, shift_y],
                preferred_element_type=jnp.float32,
            )
    return running


def convt_valid(grads, weights):
    nrow = grads.shape[0] - 2
    ncol = grads.shape[1] - 2
    running = jnp.zeros((nrow, ncol) + grads.shape[2:3] + (weights.shape[2],), jnp.float32)
    for shift_x in range(3):
        for shift_y in range(3):
            window = grads[2 - shift_x : 2 - shift_x + nrow, 2 - shift_y : 2 - shift_y + ncol]
            running = running + jnp.einsum(
                "xybo,io->xybi",
                window,
                weights[shift_x, shift_y],
                preferred_element_type=jnp.float32,
            )
    return running


def trim(values, width):
    return values[width : values.shape[0] - width, width : values.shape[1] - width]


def surrogate(logperm, observed, lift_w, lift_b, w_one, b_one, w_two, b_two, read_w):
    tile_rows, tile_cols, batch_size = logperm.shape
    both = jnp.concatenate([logperm, observed], axis=-1)
    wide = with_halo(both, ((ROW_AXES, 0), (COL_AXES, 1)), HALO)
    field = wide[..., :batch_size]
    measured = trim(wide[..., batch_size:], 2)
    mask = inside_grid(tile_rows, tile_cols, HALO)
    zero = jnp.float32(0.0)
    lifted = jnp.where(mask, field[..., None] * lift_w + lift_b, zero).astype(jnp.bfloat16)
    hidden_one = jnp.where(
        trim(mask, 1), jnp.tanh(conv_valid(lifted, w_one) + b_one), zero
    ).astype(jnp.bfloat16)
    hidden_two = jnp.tanh(conv_valid(hidden_one, w_two) + b_two)
    pressure = jnp.sum(hidden_two * read_w, axis=-1)
    misfit = pressure - measured
    grad_two = jnp.where(
        trim(mask, 2), misfit[..., None] * read_w * (1.0 - hidden_two * hidden_two), zero
    ).astype(jnp.bfloat16)
    h_one = trim(hidden_one, 2).astype(jnp.float32)
    grad_one = jnp.where(
        trim(mask, 3), convt_valid(grad_two, w_two) * (1.0 - h_one * h_one), zero
    ).astype(jnp.bfloat16)
    grad_field = jnp.sum(convt_valid(grad_one, w_one) * lift_w, axis=-1)
    return (trim(pressure, 2), grad_field)


def bit_order(sizes):
    groups = []
    low = 0
    for size in reversed(sizes):
        width = size.bit_length() - 1
        groups.append(list(range(low, low + width)))
        low += width
    core_bits, rest = groups[0], groups[1:]
    order = list(core_bits)
    depth = 0
    while any(depth < len(group) for group in rest):
        for group in rest:
            if depth < len(group):
                order.append(group[depth])
        depth += 1
    return order, low


def exchange(values, bit, count):
    pairs = [(i, i ^ (1 << bit)) for i in range(count)]
    return lax.ppermute(values, ALL_AXES, pairs)


def scatter_sum(projected, mode_block, sizes):
    order, nbits = bit_order(sizes)
    count = 1 << nbits
    me = lax.axis_index(ALL_AXES)
    data = projected.reshape((2,) * nbits + (mode_block, projected.shape[1]))
    present = list(range(nbits - 1, -1, -1))
    near, far = order[: nbits - FAR_COUNT], order[nbits - FAR_COUNT :]
    for bit in near:
        dim = present.index(bit)
        mine = (me >> bit) & 1
        keep = lax.dynamic_index_in_dim(data, mine, axis=dim, keepdims=False)
        send = lax.dynamic_index_in_dim(data, 1 - mine, axis=dim, keepdims=False)
        data = keep + exchange(send, bit, count)
        present.pop(dim)
    group = tuple(f"b{bit}" for bit in present)
    data = data.reshape((1 << len(present), mode_block, projected.shape[1]))
    data = lax.all_to_all(data, group, 0, 0, tiled=False)
    return jnp.sum(data, axis=0)


def gather_all(block, sizes):
    order, nbits = bit_order(sizes)
    count = 1 << nbits
    me = lax.axis_index(ALL_AXES)
    near, far = order[: nbits - FAR_COUNT], order[nbits - FAR_COUNT :]
    present = sorted(far, reverse=True)
    group = tuple(f"b{bit}" for bit in present)
    data = jnp.broadcast_to(block[None], (1 << len(present),) + block.shape)
    data = lax.all_to_all(data, group, 0, 0, tiled=False)
    data = data.reshape((2,) * len(present) + block.shape)
    for bit in reversed(near):
        mine = (me >> bit) & 1
        other = exchange(data, bit, count)
        low = jnp.where(mine == 0, data, other)
        high = jnp.where(mine == 0, other, data)
        dim = sum(1 for b in present if b > bit)
        data = jnp.stack([low, high], axis=dim)
        present.insert(dim, bit)
    return data.reshape(count * block.shape[0], block.shape[1])


def shards(coeffs, basis, observed, lift_w, lift_b, w_one, b_one, w_two, b_two, read_w):
    tile_rows, tile_cols, mode_count = basis.shape
    batch_size = coeffs.shape[1]
    sizes = (4, 8, 8, 2)
    flat_basis = basis.reshape(tile_rows * tile_cols, mode_count)
    logperm = jnp.dot(
        flat_basis,
        gather_all(coeffs, sizes),
        precision=lax.Precision.HIGHEST,
        preferred_element_type=jnp.float32,
    )
    logperm = logperm.reshape(tile_rows, tile_cols, batch_size)
    pressure, grad_field = surrogate(
        logperm, observed, lift_w, lift_b, w_one, b_one, w_two, b_two, read_w
    )
    grad_flat = grad_field.reshape(tile_rows * tile_cols, batch_size)
    projected = lax.dot_general(
        flat_basis,
        grad_flat,
        (((0,), (0,)), ((), ())),
        precision=lax.Precision.HIGHEST,
        preferred_element_type=jnp.float32,
    )
    summed = scatter_sum(projected, coeffs.shape[0], sizes)
    grad_coeffs = summed + prior_weight * coeffs
    return (pressure, grad_coeffs)


def solution(mesh):
    row_size, col_size = mesh.devices.shape
    fine = Mesh(mesh.devices.reshape((2,) * len(ALL_AXES)), ALL_AXES)
    return jax.shard_map(
        shards,
        mesh=fine,
        in_specs=(
            P(ALL_AXES, None),
            P(ROW_AXES, COL_AXES, None),
            P(ROW_AXES, COL_AXES, None),
            P(),
            P(),
            P(),
            P(),
            P(),
            P(),
            P(),
        ),
        out_specs=(P(ROW_AXES, COL_AXES, None), P(ALL_AXES, None)),
        check_vma=False,
    )
```

```python
import jax
import jax.numpy as jnp
from jax import lax
from jax.sharding import Mesh, PartitionSpec as P
import numpy as np

prior_weight = 0.1


ALL_AXES = tuple(f"b{bit}" for bit in range(8, -1, -1))
ROW_AXES = ALL_AXES[:5]
COL_AXES = ALL_AXES[5:]
FAR_COUNT = 5


def with_halo(block, sides, width):
    for axis, dim in sides:
        count = lax.axis_size(axis)
        forward = [(i, i + 1) for i in range(count - 1)]
        backward = [(target, source) for source, target in forward]
        low = lax.ppermute(
            lax.slice_in_dim(block, block.shape[dim] - width, None, axis=dim), axis, forward
        )
        high = lax.ppermute(lax.slice_in_dim(block, 0, width, axis=dim), axis, backward)
        block = jnp.concatenate([low, block, high], axis=dim)
    return block


HALO = 4


def inside_grid(tile_rows, tile_cols, halo):
    row_count = lax.axis_size(ROW_AXES)
    col_count = lax.axis_size(COL_AXES)
    rows = lax.axis_index(ROW_AXES) * tile_rows - halo + jnp.arange(tile_rows + 2 * halo)
    cols = lax.axis_index(COL_AXES) * tile_cols - halo + jnp.arange(tile_cols + 2 * halo)
    row_ok = (rows >= 0) & (rows < row_count * tile_rows)
    col_ok = (cols >= 0) & (cols < col_count * tile_cols)
    return (row_ok[:, None] & col_ok[None, :])[:, :, None, None]


def channels(vector):
    return vector[:, None]


def conv_valid(values, weights):
    nrow = values.shape[0] - 2
    ncol = values.shape[1] - 2
    running = jnp.zeros((nrow, ncol, weights.shape[3], values.shape[3]), jnp.float32)
    for shift_x in range(3):
        for shift_y in range(3):
            window = values[shift_x : shift_x + nrow, shift_y : shift_y + ncol]
            running = running + jnp.einsum(
                "xyib,io->xyob",
                window,
                weights[shift_x, shift_y],
                preferred_element_type=jnp.float32,
            )
    return running


def convt_valid(grads, weights):
    nrow = grads.shape[0] - 2
    ncol = grads.shape[1] - 2
    running = jnp.zeros((nrow, ncol, weights.shape[2], grads.shape[3]), jnp.float32)
    for shift_x in range(3):
        for shift_y in range(3):
            window = grads[2 - shift_x : 2 - shift_x + nrow, 2 - shift_y : 2 - shift_y + ncol]
            running = running + jnp.einsum(
                "xyob,io->xyib",
                window,
                weights[shift_x, shift_y],
                preferred_element_type=jnp.float32,
            )
    return running


def trim(values, width):
    return values[width : values.shape[0] - width, width : values.shape[1] - width]


def surrogate(logperm, observed, lift_w, lift_b, w_one, b_one, w_two, b_two, read_w):
    tile_rows, tile_cols, batch_size = logperm.shape
    both = jnp.concatenate([logperm, observed], axis=-1)
    wide = with_halo(both, ((ROW_AXES, 0), (COL_AXES, 1)), HALO)
    field = wide[..., :batch_size]
    measured = trim(wide[..., batch_size:], 2)
    mask = inside_grid(tile_rows, tile_cols, HALO)
    zero = jnp.float32(0.0)
    lifted = jnp.where(
        mask, field[:, :, None, :] * channels(lift_w) + channels(lift_b), zero
    ).astype(jnp.bfloat16)
    hidden_one = jnp.where(
        trim(mask, 1), jnp.tanh(conv_valid(lifted, w_one) + channels(b_one)), zero
    ).astype(jnp.bfloat16)
    hidden_two = jnp.tanh(conv_valid(hidden_one, w_two) + channels(b_two))
    pressure = jnp.sum(hidden_two * channels(read_w), axis=2)
    misfit = pressure - measured
    grad_two = jnp.where(
        trim(mask, 2),
        misfit[:, :, None, :] * channels(read_w) * (1.0 - hidden_two * hidden_two),
        zero,
    ).astype(jnp.bfloat16)
    h_one = trim(hidden_one, 2).astype(jnp.float32)
    grad_one = jnp.where(
        trim(mask, 3), convt_valid(grad_two, w_two) * (1.0 - h_one * h_one), zero
    ).astype(jnp.bfloat16)
    grad_field = jnp.sum(convt_valid(grad_one, w_one) * channels(lift_w), axis=2)
    return (trim(pressure, 2), grad_field)


def bit_order(sizes):
    groups = []
    low = 0
    for size in reversed(sizes):
        width = size.bit_length() - 1
        groups.append(list(range(low, low + width)))
        low += width
    core_bits, rest = groups[0], groups[1:]
    order = list(core_bits)
    depth = 0
    while any(depth < len(group) for group in rest):
        for group in rest:
            if depth < len(group):
                order.append(group[depth])
        depth += 1
    return order, low


def exchange(values, bit, count):
    pairs = [(i, i ^ (1 << bit)) for i in range(count)]
    return lax.ppermute(values, ALL_AXES, pairs)


def scatter_sum(projected, mode_block, sizes):
    order, nbits = bit_order(sizes)
    count = 1 << nbits
    me = lax.axis_index(ALL_AXES)
    data = projected.reshape((2,) * nbits + (mode_block, projected.shape[1]))
    present = list(range(nbits - 1, -1, -1))
    near, far = order[: nbits - FAR_COUNT], order[nbits - FAR_COUNT :]
    for bit in near:
        dim = present.index(bit)
        mine = (me >> bit) & 1
        keep = lax.dynamic_index_in_dim(data, mine, axis=dim, keepdims=False)
        send = lax.dynamic_index_in_dim(data, 1 - mine, axis=dim, keepdims=False)
        data = keep + exchange(send, bit, count)
        present.pop(dim)
    group = tuple(f"b{bit}" for bit in present)
    data = data.reshape((1 << len(present), mode_block, projected.shape[1]))
    data = lax.all_to_all(data, group, 0, 0, tiled=False)
    return jnp.sum(data, axis=0)


def gather_all(block, sizes):
    order, nbits = bit_order(sizes)
    count = 1 << nbits
    me = lax.axis_index(ALL_AXES)
    near, far = order[: nbits - FAR_COUNT], order[nbits - FAR_COUNT :]
    present = sorted(far, reverse=True)
    group = tuple(f"b{bit}" for bit in present)
    data = jnp.broadcast_to(block[None], (1 << len(present),) + block.shape)
    data = lax.all_to_all(data, group, 0, 0, tiled=False)
    data = data.reshape((2,) * len(present) + block.shape)
    for bit in reversed(near):
        mine = (me >> bit) & 1
        other = exchange(data, bit, count)
        low = jnp.where(mine == 0, data, other)
        high = jnp.where(mine == 0, other, data)
        dim = sum(1 for b in present if b > bit)
        data = jnp.stack([low, high], axis=dim)
        present.insert(dim, bit)
    return data.reshape(count * block.shape[0], block.shape[1])


def shards(coeffs, basis, observed, lift_w, lift_b, w_one, b_one, w_two, b_two, read_w):
    tile_rows, tile_cols, mode_count = basis.shape
    batch_size = coeffs.shape[1]
    sizes = (4, 8, 8, 2)
    flat_basis = basis.reshape(tile_rows * tile_cols, mode_count)
    logperm = jnp.dot(
        flat_basis,
        gather_all(coeffs, sizes),
        precision=lax.Precision.HIGHEST,
        preferred_element_type=jnp.float32,
    )
    logperm = logperm.reshape(tile_rows, tile_cols, batch_size)
    pressure, grad_field = surrogate(
        logperm, observed, lift_w, lift_b, w_one, b_one, w_two, b_two, read_w
    )
    grad_flat = grad_field.reshape(tile_rows * tile_cols, batch_size)
    projected = lax.dot_general(
        flat_basis,
        grad_flat,
        (((0,), (0,)), ((), ())),
        precision=lax.Precision.HIGHEST,
        preferred_element_type=jnp.float32,
    )
    summed = scatter_sum(projected, coeffs.shape[0], sizes)
    grad_coeffs = summed + prior_weight * coeffs
    return (pressure, grad_coeffs)


def solution(mesh):
    row_size, col_size = mesh.devices.shape
    fine = Mesh(mesh.devices.reshape((2,) * len(ALL_AXES)), ALL_AXES)
    return jax.shard_map(
        shards,
        mesh=fine,
        in_specs=(
            P(ALL_AXES, None),
            P(ROW_AXES, COL_AXES, None),
            P(ROW_AXES, COL_AXES, None),
            P(),
            P(),
            P(),
            P(),
            P(),
            P(),
            P(),
        ),
        out_specs=(P(ROW_AXES, COL_AXES, None), P(ALL_AXES, None)),
        check_vma=False,
    )
```

```python
import jax
import jax.numpy as jnp
from jax import lax
from jax.sharding import Mesh, PartitionSpec as P
import numpy as np

prior_weight = 0.1


ALL_AXES = tuple(f"b{bit}" for bit in range(8, -1, -1))
ROW_AXES = ALL_AXES[:5]
COL_AXES = ALL_AXES[5:]
FAR_COUNT = 5


def with_halo(block, sides, width):
    for axis, dim in sides:
        count = lax.axis_size(axis)
        forward = [(i, i + 1) for i in range(count - 1)]
        backward = [(target, source) for source, target in forward]
        low = lax.ppermute(
            lax.slice_in_dim(block, block.shape[dim] - width, None, axis=dim), axis, forward
        )
        high = lax.ppermute(lax.slice_in_dim(block, 0, width, axis=dim), axis, backward)
        block = jnp.concatenate([low, block, high], axis=dim)
    return block


HALO = 4


def inside_grid(tile_rows, tile_cols, halo):
    row_count = lax.axis_size(ROW_AXES)
    col_count = lax.axis_size(COL_AXES)
    rows = lax.axis_index(ROW_AXES) * tile_rows - halo + jnp.arange(tile_rows + 2 * halo)
    cols = lax.axis_index(COL_AXES) * tile_cols - halo + jnp.arange(tile_cols + 2 * halo)
    row_ok = (rows >= 0) & (rows < row_count * tile_rows)
    col_ok = (cols >= 0) & (cols < col_count * tile_cols)
    return (row_ok[:, None] & col_ok[None, :])[:, :, None, None]


def channels(vector):
    return vector[:, None]


def conv_valid(values, weights):
    return lax.conv_general_dilated(
        values,
        weights,
        (1, 1),
        "VALID",
        dimension_numbers=("HWCN", "HWIO", "HWCN"),
        preferred_element_type=jnp.float32,
    )


def convt_valid(grads, weights):
    return lax.conv_general_dilated(
        grads,
        jnp.flip(weights, (0, 1)),
        (1, 1),
        "VALID",
        dimension_numbers=("HWCN", "HWOI", "HWCN"),
        preferred_element_type=jnp.float32,
    )


def trim(values, width):
    return values[width : values.shape[0] - width, width : values.shape[1] - width]


def surrogate(logperm, observed, lift_w, lift_b, w_one, b_one, w_two, b_two, read_w):
    tile_rows, tile_cols, batch_size = logperm.shape
    both = jnp.concatenate([logperm, observed], axis=-1)
    wide = with_halo(both, ((ROW_AXES, 0), (COL_AXES, 1)), HALO)
    field = wide[..., :batch_size]
    measured = trim(wide[..., batch_size:], 2)
    mask = inside_grid(tile_rows, tile_cols, HALO)
    zero = jnp.float32(0.0)
    lifted = jnp.where(
        mask, field[:, :, None, :] * channels(lift_w) + channels(lift_b), zero
    ).astype(jnp.bfloat16)
    hidden_one = jnp.where(
        trim(mask, 1), jnp.tanh(conv_valid(lifted, w_one) + channels(b_one)), zero
    ).astype(jnp.bfloat16)
    hidden_two = jnp.tanh(conv_valid(hidden_one, w_two) + channels(b_two))
    pressure = jnp.sum(hidden_two * channels(read_w), axis=2)
    misfit = pressure - measured
    grad_two = jnp.where(
        trim(mask, 2),
        misfit[:, :, None, :] * channels(read_w) * (1.0 - hidden_two * hidden_two),
        zero,
    ).astype(jnp.bfloat16)
    h_one = trim(hidden_one, 2).astype(jnp.float32)
    grad_one = jnp.where(
        trim(mask, 3), convt_valid(grad_two, w_two) * (1.0 - h_one * h_one), zero
    ).astype(jnp.bfloat16)
    grad_field = jnp.sum(convt_valid(grad_one, w_one) * channels(lift_w), axis=2)
    return (trim(pressure, 2), grad_field)


def bit_order(sizes):
    groups = []
    low = 0
    for size in reversed(sizes):
        width = size.bit_length() - 1
        groups.append(list(range(low, low + width)))
        low += width
    core_bits, rest = groups[0], groups[1:]
    order = list(core_bits)
    depth = 0
    while any(depth < len(group) for group in rest):
        for group in rest:
            if depth < len(group):
                order.append(group[depth])
        depth += 1
    return order, low


def exchange(values, bit, count):
    pairs = [(i, i ^ (1 << bit)) for i in range(count)]
    return lax.ppermute(values, ALL_AXES, pairs)


def scatter_sum(projected, mode_block, sizes):
    order, nbits = bit_order(sizes)
    count = 1 << nbits
    me = lax.axis_index(ALL_AXES)
    data = projected.reshape((2,) * nbits + (mode_block, projected.shape[1]))
    present = list(range(nbits - 1, -1, -1))
    near, far = order[: nbits - FAR_COUNT], order[nbits - FAR_COUNT :]
    for bit in near:
        dim = present.index(bit)
        mine = (me >> bit) & 1
        keep = lax.dynamic_index_in_dim(data, mine, axis=dim, keepdims=False)
        send = lax.dynamic_index_in_dim(data, 1 - mine, axis=dim, keepdims=False)
        data = keep + exchange(send, bit, count)
        present.pop(dim)
    group = tuple(f"b{bit}" for bit in present)
    data = data.reshape((1 << len(present), mode_block, projected.shape[1]))
    data = lax.all_to_all(data, group, 0, 0, tiled=False)
    return jnp.sum(data, axis=0)


def gather_all(block, sizes):
    order, nbits = bit_order(sizes)
    count = 1 << nbits
    me = lax.axis_index(ALL_AXES)
    near, far = order[: nbits - FAR_COUNT], order[nbits - FAR_COUNT :]
    present = sorted(far, reverse=True)
    group = tuple(f"b{bit}" for bit in present)
    data = jnp.broadcast_to(block[None], (1 << len(present),) + block.shape)
    data = lax.all_to_all(data, group, 0, 0, tiled=False)
    data = data.reshape((2,) * len(present) + block.shape)
    for bit in reversed(near):
        mine = (me >> bit) & 1
        other = exchange(data, bit, count)
        low = jnp.where(mine == 0, data, other)
        high = jnp.where(mine == 0, other, data)
        dim = sum(1 for b in present if b > bit)
        data = jnp.stack([low, high], axis=dim)
        present.insert(dim, bit)
    return data.reshape(count * block.shape[0], block.shape[1])


def shards(coeffs, basis, observed, lift_w, lift_b, w_one, b_one, w_two, b_two, read_w):
    tile_rows, tile_cols, mode_count = basis.shape
    batch_size = coeffs.shape[1]
    sizes = (4, 8, 8, 2)
    flat_basis = basis.reshape(tile_rows * tile_cols, mode_count)
    logperm = jnp.dot(
        flat_basis,
        gather_all(coeffs, sizes),
        precision=lax.Precision.HIGHEST,
        preferred_element_type=jnp.float32,
    )
    logperm = logperm.reshape(tile_rows, tile_cols, batch_size)
    pressure, grad_field = surrogate(
        logperm, observed, lift_w, lift_b, w_one, b_one, w_two, b_two, read_w
    )
    grad_flat = grad_field.reshape(tile_rows * tile_cols, batch_size)
    projected = lax.dot_general(
        flat_basis,
        grad_flat,
        (((0,), (0,)), ((), ())),
        precision=lax.Precision.HIGHEST,
        preferred_element_type=jnp.float32,
    )
    summed = scatter_sum(projected, coeffs.shape[0], sizes)
    grad_coeffs = summed + prior_weight * coeffs
    return (pressure, grad_coeffs)


def solution(mesh):
    row_size, col_size = mesh.devices.shape
    fine = Mesh(mesh.devices.reshape((2,) * len(ALL_AXES)), ALL_AXES)
    return jax.shard_map(
        shards,
        mesh=fine,
        in_specs=(
            P(ALL_AXES, None),
            P(ROW_AXES, COL_AXES, None),
            P(ROW_AXES, COL_AXES, None),
            P(),
            P(),
            P(),
            P(),
            P(),
            P(),
            P(),
        ),
        out_specs=(P(ROW_AXES, COL_AXES, None), P(ALL_AXES, None)),
        check_vma=False,
    )
```

```python
import jax
import jax.numpy as jnp
from jax import lax
from jax.sharding import Mesh, PartitionSpec as P
import numpy as np

prior_weight = 0.1


ALL_AXES = tuple(f"b{bit}" for bit in range(8, -1, -1))
ROW_AXES = ALL_AXES[:5]
COL_AXES = ALL_AXES[5:]
FAR_COUNT = 5


def with_halo(block, sides, width):
    for axis, dim in sides:
        count = lax.axis_size(axis)
        forward = [(i, i + 1) for i in range(count - 1)]
        backward = [(target, source) for source, target in forward]
        low = lax.ppermute(
            lax.slice_in_dim(block, block.shape[dim] - width, None, axis=dim), axis, forward
        )
        high = lax.ppermute(lax.slice_in_dim(block, 0, width, axis=dim), axis, backward)
        block = jnp.concatenate([low, block, high], axis=dim)
    return block


HALO = 4


def inside_grid(tile_rows, tile_cols, halo):
    row_count = lax.axis_size(ROW_AXES)
    col_count = lax.axis_size(COL_AXES)
    rows = lax.axis_index(ROW_AXES) * tile_rows - halo + jnp.arange(tile_rows + 2 * halo)
    cols = lax.axis_index(COL_AXES) * tile_cols - halo + jnp.arange(tile_cols + 2 * halo)
    row_ok = (rows >= 0) & (rows < row_count * tile_rows)
    col_ok = (cols >= 0) & (cols < col_count * tile_cols)
    return (row_ok[:, None] & col_ok[None, :])[:, :, None, None]


def channels(vector):
    return vector[:, None]


def conv_valid(values, weights):
    return lax.conv_general_dilated(
        values,
        weights,
        (1, 1),
        "VALID",
        dimension_numbers=("HWCN", "HWIO", "HWCN"),
        preferred_element_type=jnp.float32,
    )


def convt_valid(grads, weights):
    return lax.conv_general_dilated(
        grads,
        jnp.flip(weights, (0, 1)),
        (1, 1),
        "VALID",
        dimension_numbers=("HWCN", "HWOI", "HWCN"),
        preferred_element_type=jnp.float32,
    )


def trim(values, width):
    return values[width : values.shape[0] - width, width : values.shape[1] - width]


def surrogate(logperm, observed, lift_w, lift_b, w_one, b_one, w_two, b_two, read_w):
    tile_rows, tile_cols, batch_size = logperm.shape
    both = jnp.concatenate([logperm, observed], axis=-1)
    wide = with_halo(both, ((ROW_AXES, 0), (COL_AXES, 1)), HALO)
    field = wide[..., :batch_size]
    measured = trim(wide[..., batch_size:], 2)
    mask = inside_grid(tile_rows, tile_cols, HALO)
    zero = jnp.float32(0.0)
    lifted = jnp.where(
        mask, field[:, :, None, :] * channels(lift_w) + channels(lift_b), zero
    ).astype(jnp.bfloat16)
    hidden_one = jnp.where(
        trim(mask, 1), jnp.tanh(conv_valid(lifted, w_one) + channels(b_one)), zero
    ).astype(jnp.bfloat16)
    hidden_two = jnp.tanh(conv_valid(hidden_one, w_two) + channels(b_two))
    pressure = jnp.sum(hidden_two * channels(read_w), axis=2)
    misfit = pressure - measured
    grad_two = jnp.where(
        trim(mask, 2),
        misfit[:, :, None, :] * channels(read_w) * (1.0 - hidden_two * hidden_two),
        zero,
    ).astype(jnp.bfloat16)
    h_one = trim(hidden_one, 2).astype(jnp.float32)
    grad_one = jnp.where(
        trim(mask, 3), convt_valid(grad_two, w_two) * (1.0 - h_one * h_one), zero
    ).astype(jnp.bfloat16)
    grad_field = jnp.sum(convt_valid(grad_one, w_one) * channels(lift_w), axis=2)
    return (trim(pressure, 2), grad_field)


def bit_order(sizes):
    groups = []
    low = 0
    for size in reversed(sizes):
        width = size.bit_length() - 1
        groups.append(list(range(low, low + width)))
        low += width
    core_bits, rest = groups[0], groups[1:]
    order = list(core_bits)
    depth = 0
    while any(depth < len(group) for group in rest):
        for group in rest:
            if depth < len(group):
                order.append(group[depth])
        depth += 1
    return order, low


def core_orders(near):
    swapped = list(near)
    swapped[1], swapped[2] = near[2], near[1]
    return (list(near), swapped)


def exchange(values, bits, count):
    pairs = [(i, i ^ (1 << bits[i & 1])) for i in range(count)]
    return lax.ppermute(values, ALL_AXES, pairs)


def scatter_sum(projected, mode_block, sizes):
    order, nbits = bit_order(sizes)
    count = 1 << nbits
    me = lax.axis_index(ALL_AXES)
    first_core = (me & 1) == 0
    data = projected.reshape((2,) * nbits + (mode_block, projected.shape[1]))
    near = order[: nbits - FAR_COUNT]
    orders = core_orders(near)
    presents = [list(range(nbits - 1, -1, -1)) for _ in orders]
    for step in range(len(near)):
        bits = [variant[step] for variant in orders]
        kept, sent = [], []
        for bit, present in zip(bits, presents):
            dim = present.index(bit)
            mine = (me >> bit) & 1
            kept.append(lax.dynamic_index_in_dim(data, mine, axis=dim, keepdims=False))
            sent.append(lax.dynamic_index_in_dim(data, 1 - mine, axis=dim, keepdims=False))
            present.pop(dim)
        keep = kept[0] if bits[0] == bits[1] else jnp.where(first_core, kept[0], kept[1])
        send = sent[0] if bits[0] == bits[1] else jnp.where(first_core, sent[0], sent[1])
        data = keep + exchange(send, bits, count)
    present = presents[0]
    group = tuple(f"b{bit}" for bit in present)
    data = data.reshape((1 << len(present), mode_block, projected.shape[1]))
    data = lax.all_to_all(data, group, 0, 0, tiled=False)
    return jnp.sum(data, axis=0)


def gather_all(block, sizes):
    order, nbits = bit_order(sizes)
    count = 1 << nbits
    me = lax.axis_index(ALL_AXES)
    first_core = (me & 1) == 0
    near, far = order[: nbits - FAR_COUNT], order[nbits - FAR_COUNT :]
    orders = [list(reversed(variant)) for variant in core_orders(near)]
    presents = [sorted(far, reverse=True) for _ in orders]
    group = tuple(f"b{bit}" for bit in presents[0])
    data = jnp.broadcast_to(block[None], (1 << len(presents[0]),) + block.shape)
    data = lax.all_to_all(data, group, 0, 0, tiled=False)
    data = data.reshape((2,) * len(presents[0]) + block.shape)
    for step in range(len(near)):
        bits = [variant[step] for variant in orders]
        other = exchange(data, bits, count)
        stacked = []
        for bit, present in zip(bits, presents):
            mine = (me >> bit) & 1
            low = jnp.where(mine == 0, data, other)
            high = jnp.where(mine == 0, other, data)
            dim = sum(1 for b in present if b > bit)
            stacked.append(jnp.stack([low, high], axis=dim))
            present.insert(dim, bit)
        data = stacked[0] if bits[0] == bits[1] else jnp.where(first_core, stacked[0], stacked[1])
    return data.reshape(count * block.shape[0], block.shape[1])


def shards(coeffs, basis, observed, lift_w, lift_b, w_one, b_one, w_two, b_two, read_w):
    tile_rows, tile_cols, mode_count = basis.shape
    batch_size = coeffs.shape[1]
    sizes = (4, 8, 8, 2)
    flat_basis = basis.reshape(tile_rows * tile_cols, mode_count)
    logperm = jnp.dot(
        flat_basis,
        gather_all(coeffs, sizes),
        precision=lax.Precision.HIGHEST,
        preferred_element_type=jnp.float32,
    )
    logperm = logperm.reshape(tile_rows, tile_cols, batch_size)
    pressure, grad_field = surrogate(
        logperm, observed, lift_w, lift_b, w_one, b_one, w_two, b_two, read_w
    )
    grad_flat = grad_field.reshape(tile_rows * tile_cols, batch_size)
    projected = lax.dot_general(
        flat_basis,
        grad_flat,
        (((0,), (0,)), ((), ())),
        precision=lax.Precision.HIGHEST,
        preferred_element_type=jnp.float32,
    )
    summed = scatter_sum(projected, coeffs.shape[0], sizes)
    grad_coeffs = summed + prior_weight * coeffs
    return (pressure, grad_coeffs)


def solution(mesh):
    row_size, col_size = mesh.devices.shape
    fine = Mesh(mesh.devices.reshape((2,) * len(ALL_AXES)), ALL_AXES)
    return jax.shard_map(
        shards,
        mesh=fine,
        in_specs=(
            P(ALL_AXES, None),
            P(ROW_AXES, COL_AXES, None),
            P(ROW_AXES, COL_AXES, None),
            P(),
            P(),
            P(),
            P(),
            P(),
            P(),
            P(),
        ),
        out_specs=(P(ROW_AXES, COL_AXES, None), P(ALL_AXES, None)),
        check_vma=False,
    )
```

```python
import jax
import jax.numpy as jnp
from jax import lax
from jax.sharding import Mesh, PartitionSpec as P
import numpy as np

prior_weight = 0.1


ALL_AXES = tuple(f"b{bit}" for bit in range(8, -1, -1))
ROW_AXES = ALL_AXES[:5]
COL_AXES = ALL_AXES[5:]
FAR_COUNT = 5


def with_halo(block, sides, width):
    for axis, dim in sides:
        count = lax.axis_size(axis)
        forward = [(i, i + 1) for i in range(count - 1)]
        backward = [(target, source) for source, target in forward]
        low = lax.ppermute(
            lax.slice_in_dim(block, block.shape[dim] - width, None, axis=dim), axis, forward
        )
        high = lax.ppermute(lax.slice_in_dim(block, 0, width, axis=dim), axis, backward)
        block = jnp.concatenate([low, block, high], axis=dim)
    return block


HALO = 4


def inside_grid(tile_rows, tile_cols, halo):
    row_count = lax.axis_size(ROW_AXES)
    col_count = lax.axis_size(COL_AXES)
    rows = lax.axis_index(ROW_AXES) * tile_rows - halo + jnp.arange(tile_rows + 2 * halo)
    cols = lax.axis_index(COL_AXES) * tile_cols - halo + jnp.arange(tile_cols + 2 * halo)
    row_ok = (rows >= 0) & (rows < row_count * tile_rows)
    col_ok = (cols >= 0) & (cols < col_count * tile_cols)
    return (row_ok[:, None] & col_ok[None, :])[:, :, None, None]


def channels(vector):
    return vector[:, None]


def conv_valid(values, weights):
    return lax.conv_general_dilated(
        values,
        weights,
        (1, 1),
        "VALID",
        dimension_numbers=("HWCN", "HWIO", "HWCN"),
        preferred_element_type=jnp.float32,
    )


def convt_valid(grads, weights):
    return lax.conv_general_dilated(
        grads,
        jnp.flip(weights, (0, 1)),
        (1, 1),
        "VALID",
        dimension_numbers=("HWCN", "HWOI", "HWCN"),
        preferred_element_type=jnp.float32,
    )


def trim(values, width):
    return values[width : values.shape[0] - width, width : values.shape[1] - width]


def surrogate(field, measured, lift_w, lift_b, w_one, b_one, w_two, b_two, read_w):
    tile_rows = field.shape[0] - 2 * HALO
    tile_cols = field.shape[1] - 2 * HALO
    mask = inside_grid(tile_rows, tile_cols, HALO)
    zero = jnp.float32(0.0)
    lifted = jnp.where(
        mask, field[:, :, None, :] * channels(lift_w) + channels(lift_b), zero
    ).astype(jnp.bfloat16)
    hidden_one = jnp.where(
        trim(mask, 1), jnp.tanh(conv_valid(lifted, w_one) + channels(b_one)), zero
    ).astype(jnp.bfloat16)
    hidden_two = jnp.tanh(conv_valid(hidden_one, w_two) + channels(b_two))
    pressure = jnp.sum(hidden_two * channels(read_w), axis=2)
    misfit = pressure - measured
    grad_two = jnp.where(
        trim(mask, 2),
        misfit[:, :, None, :] * channels(read_w) * (1.0 - hidden_two * hidden_two),
        zero,
    ).astype(jnp.bfloat16)
    h_one = trim(hidden_one, 2).astype(jnp.float32)
    grad_one = jnp.where(
        trim(mask, 3), convt_valid(grad_two, w_two) * (1.0 - h_one * h_one), zero
    ).astype(jnp.bfloat16)
    grad_field = jnp.sum(convt_valid(grad_one, w_one) * channels(lift_w), axis=2)
    return (trim(pressure, 2), grad_field)


def bit_order(sizes):
    groups = []
    low = 0
    for size in reversed(sizes):
        width = size.bit_length() - 1
        groups.append(list(range(low, low + width)))
        low += width
    core_bits, rest = groups[0], groups[1:]
    order = list(core_bits)
    depth = 0
    while any(depth < len(group) for group in rest):
        for group in rest:
            if depth < len(group):
                order.append(group[depth])
        depth += 1
    return order, low


def core_orders(near):
    swapped = list(near)
    swapped[1], swapped[2] = near[2], near[1]
    return (list(near), swapped)


def exchange(values, bits, count):
    pairs = [(i, i ^ (1 << bits[i & 1])) for i in range(count)]
    return lax.ppermute(values, ALL_AXES, pairs)


def scatter_sum(projected, mode_block, sizes):
    order, nbits = bit_order(sizes)
    count = 1 << nbits
    me = lax.axis_index(ALL_AXES)
    first_core = (me & 1) == 0
    data = projected.reshape((2,) * nbits + (mode_block, projected.shape[1]))
    near = order[: nbits - FAR_COUNT]
    orders = core_orders(near)
    presents = [list(range(nbits - 1, -1, -1)) for _ in orders]
    for step in range(len(near)):
        bits = [variant[step] for variant in orders]
        kept, sent = [], []
        for bit, present in zip(bits, presents):
            dim = present.index(bit)
            mine = (me >> bit) & 1
            kept.append(lax.dynamic_index_in_dim(data, mine, axis=dim, keepdims=False))
            sent.append(lax.dynamic_index_in_dim(data, 1 - mine, axis=dim, keepdims=False))
            present.pop(dim)
        keep = kept[0] if bits[0] == bits[1] else jnp.where(first_core, kept[0], kept[1])
        send = sent[0] if bits[0] == bits[1] else jnp.where(first_core, sent[0], sent[1])
        data = keep + exchange(send, bits, count)
    present = presents[0]
    group = tuple(f"b{bit}" for bit in present)
    data = data.reshape((1 << len(present), mode_block, projected.shape[1]))
    data = lax.all_to_all(data, group, 0, 0, tiled=False)
    return jnp.sum(data, axis=0)


def gather_all(block, sizes):
    order, nbits = bit_order(sizes)
    count = 1 << nbits
    me = lax.axis_index(ALL_AXES)
    first_core = (me & 1) == 0
    near, far = order[: nbits - FAR_COUNT], order[nbits - FAR_COUNT :]
    orders = [list(reversed(variant)) for variant in core_orders(near)]
    presents = [sorted(far, reverse=True) for _ in orders]
    group = tuple(f"b{bit}" for bit in presents[0])
    data = jnp.broadcast_to(block[None], (1 << len(presents[0]),) + block.shape)
    data = lax.all_to_all(data, group, 0, 0, tiled=False)
    data = data.reshape((2,) * len(presents[0]) + block.shape)
    for step in range(len(near)):
        bits = [variant[step] for variant in orders]
        other = exchange(data, bits, count)
        stacked = []
        for bit, present in zip(bits, presents):
            mine = (me >> bit) & 1
            low = jnp.where(mine == 0, data, other)
            high = jnp.where(mine == 0, other, data)
            dim = sum(1 for b in present if b > bit)
            stacked.append(jnp.stack([low, high], axis=dim))
            present.insert(dim, bit)
        data = stacked[0] if bits[0] == bits[1] else jnp.where(first_core, stacked[0], stacked[1])
    return data.reshape(count * block.shape[0], block.shape[1])


def shards(coeffs, basis, observed, lift_w, lift_b, w_one, b_one, w_two, b_two, read_w):
    tile_rows, tile_cols, mode_count = basis.shape
    batch_size = coeffs.shape[1]
    sizes = (4, 8, 8, 2)
    flat_basis = basis.reshape(tile_rows * tile_cols, mode_count)
    sides = ((ROW_AXES, 0), (COL_AXES, 1))
    wide_basis = with_halo(basis, sides, HALO)
    measured = with_halo(observed, sides, 2)
    field = jnp.dot(
        wide_basis.reshape(-1, mode_count),
        gather_all(coeffs, sizes),
        precision=lax.Precision.HIGHEST,
        preferred_element_type=jnp.float32,
    )
    field = field.reshape(wide_basis.shape[0], wide_basis.shape[1], batch_size)
    pressure, grad_field = surrogate(
        field, measured, lift_w, lift_b, w_one, b_one, w_two, b_two, read_w
    )
    grad_flat = grad_field.reshape(tile_rows * tile_cols, batch_size)
    projected = lax.dot_general(
        flat_basis,
        grad_flat,
        (((0,), (0,)), ((), ())),
        precision=lax.Precision.HIGHEST,
        preferred_element_type=jnp.float32,
    )
    summed = scatter_sum(projected, coeffs.shape[0], sizes)
    grad_coeffs = summed + prior_weight * coeffs
    return (pressure, grad_coeffs)


def solution(mesh):
    row_size, col_size = mesh.devices.shape
    fine = Mesh(mesh.devices.reshape((2,) * len(ALL_AXES)), ALL_AXES)
    return jax.shard_map(
        shards,
        mesh=fine,
        in_specs=(
            P(ALL_AXES, None),
            P(ROW_AXES, COL_AXES, None),
            P(ROW_AXES, COL_AXES, None),
            P(),
            P(),
            P(),
            P(),
            P(),
            P(),
            P(),
        ),
        out_specs=(P(ROW_AXES, COL_AXES, None), P(ALL_AXES, None)),
        check_vma=False,
    )
```

```python
import jax
import jax.numpy as jnp
from jax import lax
from jax.sharding import Mesh, PartitionSpec as P
import numpy as np

prior_weight = 0.1


ALL_AXES = tuple(f"b{bit}" for bit in range(8, -1, -1))
ROW_AXES = ALL_AXES[:5]
COL_AXES = ALL_AXES[5:]
FAR_COUNT = 6


def with_halo(block, sides, width):
    for axis, dim in sides:
        count = lax.axis_size(axis)
        forward = [(i, i + 1) for i in range(count - 1)]
        backward = [(target, source) for source, target in forward]
        low = lax.ppermute(
            lax.slice_in_dim(block, block.shape[dim] - width, None, axis=dim), axis, forward
        )
        high = lax.ppermute(lax.slice_in_dim(block, 0, width, axis=dim), axis, backward)
        block = jnp.concatenate([low, block, high], axis=dim)
    return block


HALO = 4


def inside_grid(tile_rows, tile_cols, halo):
    row_count = lax.axis_size(ROW_AXES)
    col_count = lax.axis_size(COL_AXES)
    rows = lax.axis_index(ROW_AXES) * tile_rows - halo + jnp.arange(tile_rows + 2 * halo)
    cols = lax.axis_index(COL_AXES) * tile_cols - halo + jnp.arange(tile_cols + 2 * halo)
    row_ok = (rows >= 0) & (rows < row_count * tile_rows)
    col_ok = (cols >= 0) & (cols < col_count * tile_cols)
    return (row_ok[:, None] & col_ok[None, :])[:, :, None, None]


def channels(vector):
    return vector[:, None]


def conv_valid(values, weights):
    return lax.conv_general_dilated(
        values,
        weights,
        (1, 1),
        "VALID",
        dimension_numbers=("HWCN", "HWIO", "HWCN"),
        preferred_element_type=jnp.float32,
    )


def convt_valid(grads, weights):
    return lax.conv_general_dilated(
        grads,
        jnp.flip(weights, (0, 1)),
        (1, 1),
        "VALID",
        dimension_numbers=("HWCN", "HWOI", "HWCN"),
        preferred_element_type=jnp.float32,
    )


def trim(values, width):
    return values[width : values.shape[0] - width, width : values.shape[1] - width]


def surrogate(logperm, observed, lift_w, lift_b, w_one, b_one, w_two, b_two, read_w):
    tile_rows, tile_cols, batch_size = logperm.shape
    both = jnp.concatenate([logperm, observed], axis=-1)
    wide = with_halo(both, ((ROW_AXES, 0), (COL_AXES, 1)), HALO)
    field = wide[..., :batch_size]
    measured = trim(wide[..., batch_size:], 2)
    mask = inside_grid(tile_rows, tile_cols, HALO)
    zero = jnp.float32(0.0)
    lifted = jnp.where(
        mask, field[:, :, None, :] * channels(lift_w) + channels(lift_b), zero
    ).astype(jnp.bfloat16)
    hidden_one = jnp.where(
        trim(mask, 1), jnp.tanh(conv_valid(lifted, w_one) + channels(b_one)), zero
    ).astype(jnp.bfloat16)
    hidden_two = jnp.tanh(conv_valid(hidden_one, w_two) + channels(b_two))
    pressure = jnp.sum(hidden_two * channels(read_w), axis=2)
    misfit = pressure - measured
    grad_two = jnp.where(
        trim(mask, 2),
        misfit[:, :, None, :] * channels(read_w) * (1.0 - hidden_two * hidden_two),
        zero,
    ).astype(jnp.bfloat16)
    h_one = trim(hidden_one, 2).astype(jnp.float32)
    grad_one = jnp.where(
        trim(mask, 3), convt_valid(grad_two, w_two) * (1.0 - h_one * h_one), zero
    ).astype(jnp.bfloat16)
    grad_field = jnp.sum(convt_valid(grad_one, w_one) * channels(lift_w), axis=2)
    return (trim(pressure, 2), grad_field)


def bit_order(sizes):
    groups = []
    low = 0
    for size in reversed(sizes):
        width = size.bit_length() - 1
        groups.append(list(range(low, low + width)))
        low += width
    core_bits, rest = groups[0], groups[1:]
    order = list(core_bits)
    depth = 0
    while any(depth < len(group) for group in rest):
        for group in rest:
            if depth < len(group):
                order.append(group[depth])
        depth += 1
    return order, low


def core_orders(near):
    swapped = list(near)
    swapped[1], swapped[2] = near[2], near[1]
    return (list(near), swapped)


def exchange(values, bits, count):
    pairs = [(i, i ^ (1 << bits[i & 1])) for i in range(count)]
    return lax.ppermute(values, ALL_AXES, pairs)


def scatter_sum(projected, mode_block, sizes):
    order, nbits = bit_order(sizes)
    count = 1 << nbits
    me = lax.axis_index(ALL_AXES)
    first_core = (me & 1) == 0
    data = projected.reshape((2,) * nbits + (mode_block, projected.shape[1]))
    near = order[: nbits - FAR_COUNT]
    orders = core_orders(near)
    presents = [list(range(nbits - 1, -1, -1)) for _ in orders]
    for step in range(len(near)):
        bits = [variant[step] for variant in orders]
        kept, sent = [], []
        for bit, present in zip(bits, presents):
            dim = present.index(bit)
            mine = (me >> bit) & 1
            kept.append(lax.dynamic_index_in_dim(data, mine, axis=dim, keepdims=False))
            sent.append(lax.dynamic_index_in_dim(data, 1 - mine, axis=dim, keepdims=False))
            present.pop(dim)
        keep = kept[0] if bits[0] == bits[1] else jnp.where(first_core, kept[0], kept[1])
        send = sent[0] if bits[0] == bits[1] else jnp.where(first_core, sent[0], sent[1])
        data = keep + exchange(send, bits, count)
    present = presents[0]
    group = tuple(f"b{bit}" for bit in present)
    data = data.reshape((1 << len(present), mode_block, projected.shape[1]))
    data = lax.all_to_all(data, group, 0, 0, tiled=False)
    return jnp.sum(data, axis=0)


def gather_all(block, sizes):
    order, nbits = bit_order(sizes)
    count = 1 << nbits
    me = lax.axis_index(ALL_AXES)
    first_core = (me & 1) == 0
    near, far = order[: nbits - FAR_COUNT], order[nbits - FAR_COUNT :]
    orders = [list(reversed(variant)) for variant in core_orders(near)]
    presents = [sorted(far, reverse=True) for _ in orders]
    group = tuple(f"b{bit}" for bit in presents[0])
    data = jnp.broadcast_to(block[None], (1 << len(presents[0]),) + block.shape)
    data = lax.all_to_all(data, group, 0, 0, tiled=False)
    data = data.reshape((2,) * len(presents[0]) + block.shape)
    for step in range(len(near)):
        bits = [variant[step] for variant in orders]
        other = exchange(data, bits, count)
        stacked = []
        for bit, present in zip(bits, presents):
            mine = (me >> bit) & 1
            low = jnp.where(mine == 0, data, other)
            high = jnp.where(mine == 0, other, data)
            dim = sum(1 for b in present if b > bit)
            stacked.append(jnp.stack([low, high], axis=dim))
            present.insert(dim, bit)
        data = stacked[0] if bits[0] == bits[1] else jnp.where(first_core, stacked[0], stacked[1])
    return data.reshape(count * block.shape[0], block.shape[1])


def shards(coeffs, basis, observed, lift_w, lift_b, w_one, b_one, w_two, b_two, read_w):
    tile_rows, tile_cols, mode_count = basis.shape
    batch_size = coeffs.shape[1]
    sizes = (4, 8, 8, 2)
    flat_basis = basis.reshape(tile_rows * tile_cols, mode_count)
    logperm = jnp.dot(
        flat_basis,
        gather_all(coeffs, sizes),
        precision=lax.Precision.HIGHEST,
        preferred_element_type=jnp.float32,
    )
    logperm = logperm.reshape(tile_rows, tile_cols, batch_size)
    pressure, grad_field = surrogate(
        logperm, observed, lift_w, lift_b, w_one, b_one, w_two, b_two, read_w
    )
    grad_flat = grad_field.reshape(tile_rows * tile_cols, batch_size)
    projected = lax.dot_general(
        flat_basis,
        grad_flat,
        (((0,), (0,)), ((), ())),
        precision=lax.Precision.HIGHEST,
        preferred_element_type=jnp.float32,
    )
    summed = scatter_sum(projected, coeffs.shape[0], sizes)
    grad_coeffs = summed + prior_weight * coeffs
    return (pressure, grad_coeffs)


def solution(mesh):
    row_size, col_size = mesh.devices.shape
    fine = Mesh(mesh.devices.reshape((2,) * len(ALL_AXES)), ALL_AXES)
    return jax.shard_map(
        shards,
        mesh=fine,
        in_specs=(
            P(ALL_AXES, None),
            P(ROW_AXES, COL_AXES, None),
            P(ROW_AXES, COL_AXES, None),
            P(),
            P(),
            P(),
            P(),
            P(),
            P(),
            P(),
        ),
        out_specs=(P(ROW_AXES, COL_AXES, None), P(ALL_AXES, None)),
        check_vma=False,
    )
```

```python
import jax
import jax.numpy as jnp
from jax import lax
from jax.sharding import Mesh, PartitionSpec as P
import numpy as np

prior_weight = 0.1


ALL_AXES = tuple(f"b{bit}" for bit in range(8, -1, -1))
ROW_AXES = ALL_AXES[:5]
COL_AXES = ALL_AXES[5:]
FAR_COUNT = 6


def with_halo(block, sides, width):
    for axis, dim in sides:
        count = lax.axis_size(axis)
        forward = [(i, i + 1) for i in range(count - 1)]
        backward = [(target, source) for source, target in forward]
        low = lax.ppermute(
            lax.slice_in_dim(block, block.shape[dim] - width, None, axis=dim), axis, forward
        )
        high = lax.ppermute(lax.slice_in_dim(block, 0, width, axis=dim), axis, backward)
        block = jnp.concatenate([low, block, high], axis=dim)
    return block


HALO = 4


def inside_grid(tile_rows, tile_cols, halo):
    row_count = lax.axis_size(ROW_AXES)
    col_count = lax.axis_size(COL_AXES)
    rows = lax.axis_index(ROW_AXES) * tile_rows - halo + jnp.arange(tile_rows + 2 * halo)
    cols = lax.axis_index(COL_AXES) * tile_cols - halo + jnp.arange(tile_cols + 2 * halo)
    row_ok = (rows >= 0) & (rows < row_count * tile_rows)
    col_ok = (cols >= 0) & (cols < col_count * tile_cols)
    return (row_ok[:, None] & col_ok[None, :])[:, :, None, None]


def channels(vector):
    return vector[:, None]


def conv_valid(values, weights):
    return lax.conv_general_dilated(
        values,
        weights,
        (1, 1),
        "VALID",
        dimension_numbers=("HWCN", "HWIO", "HWCN"),
        preferred_element_type=jnp.float32,
    )


def convt_valid(grads, weights):
    return lax.conv_general_dilated(
        grads,
        jnp.flip(weights, (0, 1)),
        (1, 1),
        "VALID",
        dimension_numbers=("HWCN", "HWOI", "HWCN"),
        preferred_element_type=jnp.float32,
    )


def trim(values, width):
    return values[width : values.shape[0] - width, width : values.shape[1] - width]


def surrogate(logperm, observed, lift_w, lift_b, w_one, b_one, w_two, b_two, read_w):
    tile_rows, tile_cols, batch_size = logperm.shape
    both = jnp.concatenate([logperm, observed], axis=-1)
    wide = with_halo(both, ((ROW_AXES, 0), (COL_AXES, 1)), HALO)
    field = wide[..., :batch_size]
    measured = trim(wide[..., batch_size:], 2)
    mask = inside_grid(tile_rows, tile_cols, HALO)
    zero = jnp.float32(0.0)
    lifted = jnp.where(
        mask, field[:, :, None, :] * channels(lift_w) + channels(lift_b), zero
    ).astype(jnp.bfloat16)
    hidden_one = jnp.where(
        trim(mask, 1), jnp.tanh(conv_valid(lifted, w_one) + channels(b_one)), zero
    ).astype(jnp.bfloat16)
    hidden_two = jnp.tanh(conv_valid(hidden_one, w_two) + channels(b_two))
    pressure = jnp.sum(hidden_two * channels(read_w), axis=2)
    misfit = pressure - measured
    grad_two = jnp.where(
        trim(mask, 2),
        misfit[:, :, None, :] * channels(read_w) * (1.0 - hidden_two * hidden_two),
        zero,
    ).astype(jnp.bfloat16)
    h_one = trim(hidden_one, 2).astype(jnp.float32)
    grad_one = jnp.where(
        trim(mask, 3), convt_valid(grad_two, w_two) * (1.0 - h_one * h_one), zero
    ).astype(jnp.bfloat16)
    grad_field = jnp.sum(convt_valid(grad_one, w_one) * channels(lift_w), axis=2)
    return (trim(pressure, 2), grad_field)


def bit_order(sizes):
    groups = []
    low = 0
    for size in reversed(sizes):
        width = size.bit_length() - 1
        groups.append(list(range(low, low + width)))
        low += width
    core_bits, rest = groups[0], groups[1:]
    order = list(core_bits)
    depth = 0
    while any(depth < len(group) for group in rest):
        for group in rest:
            if depth < len(group):
                order.append(group[depth])
        depth += 1
    return order, low


def core_orders(near):
    swapped = list(near)
    swapped[1], swapped[2] = near[2], near[1]
    return (list(near), swapped)


def far_groups(present):
    longest = [bit for bit in present if bit in (8, 6, 3)]
    return [[bit for bit in present if bit not in longest], longest]


def exchange(values, bits, count):
    pairs = [(i, i ^ (1 << bits[i & 1])) for i in range(count)]
    return lax.ppermute(values, ALL_AXES, pairs)


def scatter_sum(projected, mode_block, sizes):
    order, nbits = bit_order(sizes)
    count = 1 << nbits
    me = lax.axis_index(ALL_AXES)
    first_core = (me & 1) == 0
    data = projected.reshape((2,) * nbits + (mode_block, projected.shape[1]))
    near = order[: nbits - FAR_COUNT]
    orders = core_orders(near)
    presents = [list(range(nbits - 1, -1, -1)) for _ in orders]
    for step in range(len(near)):
        bits = [variant[step] for variant in orders]
        kept, sent = [], []
        for bit, present in zip(bits, presents):
            dim = present.index(bit)
            mine = (me >> bit) & 1
            kept.append(lax.dynamic_index_in_dim(data, mine, axis=dim, keepdims=False))
            sent.append(lax.dynamic_index_in_dim(data, 1 - mine, axis=dim, keepdims=False))
            present.pop(dim)
        keep = kept[0] if bits[0] == bits[1] else jnp.where(first_core, kept[0], kept[1])
        send = sent[0] if bits[0] == bits[1] else jnp.where(first_core, sent[0], sent[1])
        data = keep + exchange(send, bits, count)
    present = presents[0]
    for group_bits in far_groups(present):
        others = [bit for bit in present if bit not in group_bits]
        data = jnp.transpose(
            data,
            [present.index(bit) for bit in group_bits + others]
            + [len(present), len(present) + 1],
        )
        data = data.reshape((1 << len(group_bits), -1, mode_block, projected.shape[1]))
        data = lax.all_to_all(data, tuple(f"b{bit}" for bit in group_bits), 0, 0, tiled=False)
        data = jnp.sum(data, axis=0).reshape((2,) * len(others) + (mode_block, projected.shape[1]))
        present = others
    return data.reshape(mode_block, projected.shape[1])


def gather_all(block, sizes):
    order, nbits = bit_order(sizes)
    count = 1 << nbits
    me = lax.axis_index(ALL_AXES)
    first_core = (me & 1) == 0
    near, far = order[: nbits - FAR_COUNT], order[nbits - FAR_COUNT :]
    orders = [list(reversed(variant)) for variant in core_orders(near)]
    present = []
    data = block
    for group_bits in reversed(far_groups(sorted(far, reverse=True))):
        data = jnp.broadcast_to(data[None], (1 << len(group_bits),) + data.shape)
        data = lax.all_to_all(data, tuple(f"b{bit}" for bit in group_bits), 0, 0, tiled=False)
        data = data.reshape((2,) * len(group_bits) + data.shape[1:])
        present = group_bits + present
    ranked = sorted(present, reverse=True)
    data = jnp.transpose(
        data, [present.index(bit) for bit in ranked] + [len(present), len(present) + 1]
    )
    presents = [list(ranked) for _ in orders]
    for step in range(len(near)):
        bits = [variant[step] for variant in orders]
        other = exchange(data, bits, count)
        stacked = []
        for bit, present in zip(bits, presents):
            mine = (me >> bit) & 1
            low = jnp.where(mine == 0, data, other)
            high = jnp.where(mine == 0, other, data)
            dim = sum(1 for b in present if b > bit)
            stacked.append(jnp.stack([low, high], axis=dim))
            present.insert(dim, bit)
        data = stacked[0] if bits[0] == bits[1] else jnp.where(first_core, stacked[0], stacked[1])
    return data.reshape(count * block.shape[0], block.shape[1])


def shards(coeffs, basis, observed, lift_w, lift_b, w_one, b_one, w_two, b_two, read_w):
    tile_rows, tile_cols, mode_count = basis.shape
    batch_size = coeffs.shape[1]
    sizes = (4, 8, 8, 2)
    flat_basis = basis.reshape(tile_rows * tile_cols, mode_count)
    logperm = jnp.dot(
        flat_basis,
        gather_all(coeffs, sizes),
        precision=lax.Precision.HIGHEST,
        preferred_element_type=jnp.float32,
    )
    logperm = logperm.reshape(tile_rows, tile_cols, batch_size)
    pressure, grad_field = surrogate(
        logperm, observed, lift_w, lift_b, w_one, b_one, w_two, b_two, read_w
    )
    grad_flat = grad_field.reshape(tile_rows * tile_cols, batch_size)
    projected = lax.dot_general(
        flat_basis,
        grad_flat,
        (((0,), (0,)), ((), ())),
        precision=lax.Precision.HIGHEST,
        preferred_element_type=jnp.float32,
    )
    summed = scatter_sum(projected, coeffs.shape[0], sizes)
    grad_coeffs = summed + prior_weight * coeffs
    return (pressure, grad_coeffs)


def solution(mesh):
    row_size, col_size = mesh.devices.shape
    fine = Mesh(mesh.devices.reshape((2,) * len(ALL_AXES)), ALL_AXES)
    return jax.shard_map(
        shards,
        mesh=fine,
        in_specs=(
            P(ALL_AXES, None),
            P(ROW_AXES, COL_AXES, None),
            P(ROW_AXES, COL_AXES, None),
            P(),
            P(),
            P(),
            P(),
            P(),
            P(),
            P(),
        ),
        out_specs=(P(ROW_AXES, COL_AXES, None), P(ALL_AXES, None)),
        check_vma=False,
    )
```

```python
import jax
import jax.numpy as jnp
from jax import lax
from jax.sharding import Mesh, PartitionSpec as P
import numpy as np

prior_weight = 0.1


ALL_AXES = tuple(f"b{bit}" for bit in range(8, -1, -1))
ROW_AXES = ALL_AXES[:5]
COL_AXES = ALL_AXES[5:]
FAR_COUNT = 7


def with_halo(block, sides, width):
    for axis, dim in sides:
        count = lax.axis_size(axis)
        forward = [(i, i + 1) for i in range(count - 1)]
        backward = [(target, source) for source, target in forward]
        low = lax.ppermute(
            lax.slice_in_dim(block, block.shape[dim] - width, None, axis=dim), axis, forward
        )
        high = lax.ppermute(lax.slice_in_dim(block, 0, width, axis=dim), axis, backward)
        block = jnp.concatenate([low, block, high], axis=dim)
    return block


HALO = 4


def inside_grid(tile_rows, tile_cols, halo):
    row_count = lax.axis_size(ROW_AXES)
    col_count = lax.axis_size(COL_AXES)
    rows = lax.axis_index(ROW_AXES) * tile_rows - halo + jnp.arange(tile_rows + 2 * halo)
    cols = lax.axis_index(COL_AXES) * tile_cols - halo + jnp.arange(tile_cols + 2 * halo)
    row_ok = (rows >= 0) & (rows < row_count * tile_rows)
    col_ok = (cols >= 0) & (cols < col_count * tile_cols)
    return (row_ok[:, None] & col_ok[None, :])[:, :, None, None]


def channels(vector):
    return vector[:, None]


def conv_valid(values, weights):
    return lax.conv_general_dilated(
        values,
        weights,
        (1, 1),
        "VALID",
        dimension_numbers=("HWCN", "HWIO", "HWCN"),
        preferred_element_type=jnp.float32,
    )


def convt_valid(grads, weights):
    return lax.conv_general_dilated(
        grads,
        jnp.flip(weights, (0, 1)),
        (1, 1),
        "VALID",
        dimension_numbers=("HWCN", "HWOI", "HWCN"),
        preferred_element_type=jnp.float32,
    )


def trim(values, width):
    return values[width : values.shape[0] - width, width : values.shape[1] - width]


def surrogate(logperm, observed, lift_w, lift_b, w_one, b_one, w_two, b_two, read_w):
    tile_rows, tile_cols, batch_size = logperm.shape
    both = jnp.concatenate([logperm, observed], axis=-1)
    wide = with_halo(both, ((ROW_AXES, 0), (COL_AXES, 1)), HALO)
    field = wide[..., :batch_size]
    measured = trim(wide[..., batch_size:], 2)
    mask = inside_grid(tile_rows, tile_cols, HALO)
    zero = jnp.float32(0.0)
    lifted = jnp.where(
        mask, field[:, :, None, :] * channels(lift_w) + channels(lift_b), zero
    ).astype(jnp.bfloat16)
    hidden_one = jnp.where(
        trim(mask, 1), jnp.tanh(conv_valid(lifted, w_one) + channels(b_one)), zero
    ).astype(jnp.bfloat16)
    hidden_two = jnp.tanh(conv_valid(hidden_one, w_two) + channels(b_two))
    pressure = jnp.sum(hidden_two * channels(read_w), axis=2)
    misfit = pressure - measured
    grad_two = jnp.where(
        trim(mask, 2),
        misfit[:, :, None, :] * channels(read_w) * (1.0 - hidden_two * hidden_two),
        zero,
    ).astype(jnp.bfloat16)
    h_one = trim(hidden_one, 2).astype(jnp.float32)
    grad_one = jnp.where(
        trim(mask, 3), convt_valid(grad_two, w_two) * (1.0 - h_one * h_one), zero
    ).astype(jnp.bfloat16)
    grad_field = jnp.sum(convt_valid(grad_one, w_one) * channels(lift_w), axis=2)
    return (trim(pressure, 2), grad_field)


def bit_order(sizes):
    groups = []
    low = 0
    for size in reversed(sizes):
        width = size.bit_length() - 1
        groups.append(list(range(low, low + width)))
        low += width
    core_bits, rest = groups[0], groups[1:]
    order = list(core_bits)
    depth = 0
    while any(depth < len(group) for group in rest):
        for group in rest:
            if depth < len(group):
                order.append(group[depth])
        depth += 1
    return order, low


def core_orders(near):
    swapped = list(near)
    if len(near) > 2:
        swapped[1], swapped[2] = near[2], near[1]
    return (list(near), swapped)


def exchange(values, bits, count):
    pairs = [(i, i ^ (1 << bits[i & 1])) for i in range(count)]
    return lax.ppermute(values, ALL_AXES, pairs)


def scatter_sum(projected, mode_block, sizes):
    order, nbits = bit_order(sizes)
    count = 1 << nbits
    me = lax.axis_index(ALL_AXES)
    first_core = (me & 1) == 0
    data = projected.reshape((2,) * nbits + (mode_block, projected.shape[1]))
    near = order[: nbits - FAR_COUNT]
    orders = core_orders(near)
    presents = [list(range(nbits - 1, -1, -1)) for _ in orders]
    for step in range(len(near)):
        bits = [variant[step] for variant in orders]
        kept, sent = [], []
        for bit, present in zip(bits, presents):
            dim = present.index(bit)
            mine = (me >> bit) & 1
            kept.append(lax.dynamic_index_in_dim(data, mine, axis=dim, keepdims=False))
            sent.append(lax.dynamic_index_in_dim(data, 1 - mine, axis=dim, keepdims=False))
            present.pop(dim)
        keep = kept[0] if bits[0] == bits[1] else jnp.where(first_core, kept[0], kept[1])
        send = sent[0] if bits[0] == bits[1] else jnp.where(first_core, sent[0], sent[1])
        data = keep + exchange(send, bits, count)
    present = presents[0]
    group = tuple(f"b{bit}" for bit in present)
    data = data.reshape((1 << len(present), mode_block, projected.shape[1]))
    data = lax.all_to_all(data, group, 0, 0, tiled=False)
    return jnp.sum(data, axis=0)


def gather_all(block, sizes):
    order, nbits = bit_order(sizes)
    count = 1 << nbits
    me = lax.axis_index(ALL_AXES)
    first_core = (me & 1) == 0
    near, far = order[: nbits - FAR_COUNT], order[nbits - FAR_COUNT :]
    orders = [list(reversed(variant)) for variant in core_orders(near)]
    presents = [sorted(far, reverse=True) for _ in orders]
    group = tuple(f"b{bit}" for bit in presents[0])
    data = jnp.broadcast_to(block[None], (1 << len(presents[0]),) + block.shape)
    data = lax.all_to_all(data, group, 0, 0, tiled=False)
    data = data.reshape((2,) * len(presents[0]) + block.shape)
    for step in range(len(near)):
        bits = [variant[step] for variant in orders]
        other = exchange(data, bits, count)
        stacked = []
        for bit, present in zip(bits, presents):
            mine = (me >> bit) & 1
            low = jnp.where(mine == 0, data, other)
            high = jnp.where(mine == 0, other, data)
            dim = sum(1 for b in present if b > bit)
            stacked.append(jnp.stack([low, high], axis=dim))
            present.insert(dim, bit)
        data = stacked[0] if bits[0] == bits[1] else jnp.where(first_core, stacked[0], stacked[1])
    return data.reshape(count * block.shape[0], block.shape[1])


def shards(coeffs, basis, observed, lift_w, lift_b, w_one, b_one, w_two, b_two, read_w):
    tile_rows, tile_cols, mode_count = basis.shape
    batch_size = coeffs.shape[1]
    sizes = (4, 8, 8, 2)
    flat_basis = basis.reshape(tile_rows * tile_cols, mode_count)
    logperm = jnp.dot(
        flat_basis,
        gather_all(coeffs, sizes),
        precision=lax.Precision.HIGHEST,
        preferred_element_type=jnp.float32,
    )
    logperm = logperm.reshape(tile_rows, tile_cols, batch_size)
    pressure, grad_field = surrogate(
        logperm, observed, lift_w, lift_b, w_one, b_one, w_two, b_two, read_w
    )
    grad_flat = grad_field.reshape(tile_rows * tile_cols, batch_size)
    projected = lax.dot_general(
        flat_basis,
        grad_flat,
        (((0,), (0,)), ((), ())),
        precision=lax.Precision.HIGHEST,
        preferred_element_type=jnp.float32,
    )
    summed = scatter_sum(projected, coeffs.shape[0], sizes)
    grad_coeffs = summed + prior_weight * coeffs
    return (pressure, grad_coeffs)


def solution(mesh):
    row_size, col_size = mesh.devices.shape
    fine = Mesh(mesh.devices.reshape((2,) * len(ALL_AXES)), ALL_AXES)
    return jax.shard_map(
        shards,
        mesh=fine,
        in_specs=(
            P(ALL_AXES, None),
            P(ROW_AXES, COL_AXES, None),
            P(ROW_AXES, COL_AXES, None),
            P(),
            P(),
            P(),
            P(),
            P(),
            P(),
            P(),
        ),
        out_specs=(P(ROW_AXES, COL_AXES, None), P(ALL_AXES, None)),
        check_vma=False,
    )
```

```python
import jax
import jax.numpy as jnp
from jax import lax
from jax.sharding import Mesh, PartitionSpec as P
from jax.experimental.layout import Layout, with_layout_constraint
import numpy as np

prior_weight = 0.1


ALL_AXES = tuple(f"b{bit}" for bit in range(8, -1, -1))
ROW_AXES = ALL_AXES[:5]
COL_AXES = ALL_AXES[5:]
FAR_COUNT = 6


def with_halo(block, sides, width):
    for axis, dim in sides:
        count = lax.axis_size(axis)
        forward = [(i, i + 1) for i in range(count - 1)]
        backward = [(target, source) for source, target in forward]
        low = lax.ppermute(
            lax.slice_in_dim(block, block.shape[dim] - width, None, axis=dim), axis, forward
        )
        high = lax.ppermute(lax.slice_in_dim(block, 0, width, axis=dim), axis, backward)
        block = jnp.concatenate([low, block, high], axis=dim)
    return block


HALO = 4


def inside_grid(tile_rows, tile_cols, halo):
    row_count = lax.axis_size(ROW_AXES)
    col_count = lax.axis_size(COL_AXES)
    rows = lax.axis_index(ROW_AXES) * tile_rows - halo + jnp.arange(tile_rows + 2 * halo)
    cols = lax.axis_index(COL_AXES) * tile_cols - halo + jnp.arange(tile_cols + 2 * halo)
    row_ok = (rows >= 0) & (rows < row_count * tile_rows)
    col_ok = (cols >= 0) & (cols < col_count * tile_cols)
    return (row_ok[:, None] & col_ok[None, :])[:, :, None, None]


def channels(vector):
    return vector[:, None]


def conv_valid(values, weights):
    return lax.conv_general_dilated(
        values,
        weights,
        (1, 1),
        "VALID",
        dimension_numbers=("HWCN", "HWIO", "HWCN"),
        preferred_element_type=jnp.float32,
    )


def convt_valid(grads, weights):
    return lax.conv_general_dilated(
        grads,
        jnp.flip(weights, (0, 1)),
        (1, 1),
        "VALID",
        dimension_numbers=("HWCN", "HWOI", "HWCN"),
        preferred_element_type=jnp.float32,
    )


def trim(values, width):
    return values[width : values.shape[0] - width, width : values.shape[1] - width]


def surrogate(logperm, observed, lift_w, lift_b, w_one, b_one, w_two, b_two, read_w):
    tile_rows, tile_cols, batch_size = logperm.shape
    both = jnp.concatenate([logperm, observed], axis=-1)
    wide = with_halo(both, ((ROW_AXES, 0), (COL_AXES, 1)), HALO)
    field = wide[..., :batch_size]
    measured = trim(wide[..., batch_size:], 2)
    mask = inside_grid(tile_rows, tile_cols, HALO)
    zero = jnp.float32(0.0)
    lifted = jnp.where(
        mask, field[:, :, None, :] * channels(lift_w) + channels(lift_b), zero
    ).astype(jnp.bfloat16)
    hidden_one = jnp.where(
        trim(mask, 1), jnp.tanh(conv_valid(lifted, w_one) + channels(b_one)), zero
    ).astype(jnp.bfloat16)
    hidden_two = jnp.tanh(conv_valid(hidden_one, w_two) + channels(b_two))
    pressure = jnp.sum(hidden_two * channels(read_w), axis=2)
    misfit = pressure - measured
    grad_two = jnp.where(
        trim(mask, 2),
        misfit[:, :, None, :] * channels(read_w) * (1.0 - hidden_two * hidden_two),
        zero,
    ).astype(jnp.bfloat16)
    h_one = trim(hidden_one, 2).astype(jnp.float32)
    grad_one = jnp.where(
        trim(mask, 3), convt_valid(grad_two, w_two) * (1.0 - h_one * h_one), zero
    ).astype(jnp.bfloat16)
    grad_field = jnp.sum(convt_valid(grad_one, w_one) * channels(lift_w), axis=2)
    return (trim(pressure, 2), grad_field)


def bit_order(sizes):
    groups = []
    low = 0
    for size in reversed(sizes):
        width = size.bit_length() - 1
        groups.append(list(range(low, low + width)))
        low += width
    core_bits, rest = groups[0], groups[1:]
    order = list(core_bits)
    depth = 0
    while any(depth < len(group) for group in rest):
        for group in rest:
            if depth < len(group):
                order.append(group[depth])
        depth += 1
    return order, low


def core_orders(near):
    swapped = list(near)
    swapped[1], swapped[2] = near[2], near[1]
    return (list(near), swapped)


def exchange(values, bits, count):
    pairs = [(i, i ^ (1 << bits[i & 1])) for i in range(count)]
    return lax.ppermute(values, ALL_AXES, pairs)


def scatter_sum(projected, mode_block, sizes):
    order, nbits = bit_order(sizes)
    count = 1 << nbits
    me = lax.axis_index(ALL_AXES)
    first_core = (me & 1) == 0
    data = projected.reshape((2,) * nbits + (mode_block, projected.shape[1]))
    near = order[: nbits - FAR_COUNT]
    orders = core_orders(near)
    presents = [list(range(nbits - 1, -1, -1)) for _ in orders]
    for step in range(len(near)):
        bits = [variant[step] for variant in orders]
        kept, sent = [], []
        for bit, present in zip(bits, presents):
            dim = present.index(bit)
            mine = (me >> bit) & 1
            kept.append(lax.dynamic_index_in_dim(data, mine, axis=dim, keepdims=False))
            sent.append(lax.dynamic_index_in_dim(data, 1 - mine, axis=dim, keepdims=False))
            present.pop(dim)
        keep = kept[0] if bits[0] == bits[1] else jnp.where(first_core, kept[0], kept[1])
        send = sent[0] if bits[0] == bits[1] else jnp.where(first_core, sent[0], sent[1])
        data = keep + exchange(send, bits, count)
    present = presents[0]
    group = tuple(f"b{bit}" for bit in present)
    data = data.reshape((1 << len(present), mode_block, projected.shape[1]))
    data = lax.all_to_all(data, group, 0, 0, tiled=False)
    return jnp.sum(data, axis=0)


def gather_all(block, sizes):
    order, nbits = bit_order(sizes)
    count = 1 << nbits
    me = lax.axis_index(ALL_AXES)
    first_core = (me & 1) == 0
    near, far = order[: nbits - FAR_COUNT], order[nbits - FAR_COUNT :]
    orders = [list(reversed(variant)) for variant in core_orders(near)]
    presents = [sorted(far, reverse=True) for _ in orders]
    group = tuple(f"b{bit}" for bit in presents[0])
    data = jnp.broadcast_to(block[None], (1 << len(presents[0]),) + block.shape)
    data = lax.all_to_all(data, group, 0, 0, tiled=False)
    data = data.reshape((2,) * len(presents[0]) + block.shape)
    for step in range(len(near)):
        bits = [variant[step] for variant in orders]
        other = exchange(data, bits, count)
        stacked = []
        for bit, present in zip(bits, presents):
            mine = (me >> bit) & 1
            low = jnp.where(mine == 0, data, other)
            high = jnp.where(mine == 0, other, data)
            dim = sum(1 for b in present if b > bit)
            stacked.append(jnp.stack([low, high], axis=dim))
            present.insert(dim, bit)
        data = stacked[0] if bits[0] == bits[1] else jnp.where(first_core, stacked[0], stacked[1])
    return data.reshape(count * block.shape[0], block.shape[1])


def shards(coeffs, basis, observed, lift_w, lift_b, w_one, b_one, w_two, b_two, read_w):
    tile_rows, tile_cols, mode_count = basis.shape
    batch_size = coeffs.shape[1]
    sizes = (4, 8, 8, 2)
    flat_basis = basis.reshape(tile_rows * tile_cols, mode_count)
    logperm = jnp.dot(
        flat_basis,
        gather_all(coeffs, sizes),
        precision=lax.Precision.HIGHEST,
        preferred_element_type=jnp.float32,
    )
    logperm = logperm.reshape(tile_rows, tile_cols, batch_size)
    pressure, grad_field = surrogate(
        logperm, observed, lift_w, lift_b, w_one, b_one, w_two, b_two, read_w
    )
    grad_flat = grad_field.reshape(tile_rows * tile_cols, batch_size)
    projected = lax.dot_general(
        flat_basis,
        grad_flat,
        (((0,), (0,)), ((), ())),
        precision=lax.Precision.HIGHEST,
        preferred_element_type=jnp.float32,
    )
    projected = with_layout_constraint(projected, Layout(major_to_minor=(0, 1)))
    summed = scatter_sum(projected, coeffs.shape[0], sizes)
    grad_coeffs = summed + prior_weight * coeffs
    return (pressure, grad_coeffs)


def solution(mesh):
    row_size, col_size = mesh.devices.shape
    fine = Mesh(mesh.devices.reshape((2,) * len(ALL_AXES)), ALL_AXES)
    return jax.shard_map(
        shards,
        mesh=fine,
        in_specs=(
            P(ALL_AXES, None),
            P(ROW_AXES, COL_AXES, None),
            P(ROW_AXES, COL_AXES, None),
            P(),
            P(),
            P(),
            P(),
            P(),
            P(),
            P(),
        ),
        out_specs=(P(ROW_AXES, COL_AXES, None), P(ALL_AXES, None)),
        check_vma=False,
    )
```

```python
import jax
import jax.numpy as jnp
from jax import lax
from jax.sharding import Mesh, PartitionSpec as P
from jax.experimental.layout import Layout, with_layout_constraint
import numpy as np

prior_weight = 0.1


ALL_AXES = tuple(f"b{bit}" for bit in range(8, -1, -1))
ROW_AXES = ALL_AXES[:5]
COL_AXES = ALL_AXES[5:]
FAR_COUNT = 6


def with_halo(block, sides, width):
    for axis, dim in sides:
        count = lax.axis_size(axis)
        forward = [(i, i + 1) for i in range(count - 1)]
        backward = [(target, source) for source, target in forward]
        low = lax.ppermute(
            lax.slice_in_dim(block, block.shape[dim] - width, None, axis=dim), axis, forward
        )
        high = lax.ppermute(lax.slice_in_dim(block, 0, width, axis=dim), axis, backward)
        block = jnp.concatenate([low, block, high], axis=dim)
    return block


HALO = 4


def inside_grid(tile_rows, tile_cols, halo):
    row_count = lax.axis_size(ROW_AXES)
    col_count = lax.axis_size(COL_AXES)
    rows = lax.axis_index(ROW_AXES) * tile_rows - halo + jnp.arange(tile_rows + 2 * halo)
    cols = lax.axis_index(COL_AXES) * tile_cols - halo + jnp.arange(tile_cols + 2 * halo)
    row_ok = (rows >= 0) & (rows < row_count * tile_rows)
    col_ok = (cols >= 0) & (cols < col_count * tile_cols)
    return (row_ok[:, None] & col_ok[None, :])[:, :, None, None]


def channels(vector):
    return vector[:, None]


def conv_valid(values, weights):
    return lax.conv_general_dilated(
        values,
        weights,
        (1, 1),
        "VALID",
        dimension_numbers=("HWCN", "HWIO", "HWCN"),
        preferred_element_type=jnp.float32,
    )


def convt_valid(grads, weights):
    return lax.conv_general_dilated(
        grads,
        jnp.flip(weights, (0, 1)),
        (1, 1),
        "VALID",
        dimension_numbers=("HWCN", "HWOI", "HWCN"),
        preferred_element_type=jnp.float32,
    )


def trim(values, width):
    return values[width : values.shape[0] - width, width : values.shape[1] - width]


def surrogate(logperm, observed, lift_w, lift_b, w_one, b_one, w_two, b_two, read_w):
    tile_rows, tile_cols, batch_size = logperm.shape
    both = jnp.concatenate([logperm, observed], axis=-1)
    wide = with_halo(both, ((ROW_AXES, 0), (COL_AXES, 1)), HALO)
    field = wide[..., :batch_size]
    measured = trim(wide[..., batch_size:], 2)
    mask = inside_grid(tile_rows, tile_cols, HALO)
    zero = jnp.float32(0.0)
    lifted = jnp.where(
        mask, field[:, :, None, :] * channels(lift_w) + channels(lift_b), zero
    ).astype(jnp.bfloat16)
    hidden_one = jnp.where(
        trim(mask, 1), jnp.tanh(conv_valid(lifted, w_one) + channels(b_one)), zero
    ).astype(jnp.bfloat16)
    hidden_two = jnp.tanh(conv_valid(hidden_one, w_two) + channels(b_two))
    pressure = jnp.sum(hidden_two * channels(read_w), axis=2)
    misfit = pressure - measured
    grad_two = jnp.where(
        trim(mask, 2),
        misfit[:, :, None, :] * channels(read_w) * (1.0 - hidden_two * hidden_two),
        zero,
    ).astype(jnp.bfloat16)
    h_one = trim(hidden_one, 2).astype(jnp.float32)
    grad_one = jnp.where(
        trim(mask, 3), convt_valid(grad_two, w_two) * (1.0 - h_one * h_one), zero
    ).astype(jnp.bfloat16)
    grad_field = jnp.sum(convt_valid(grad_one, w_one) * channels(lift_w), axis=2)
    return (trim(pressure, 2), grad_field)


def bit_order(sizes):
    groups = []
    low = 0
    for size in reversed(sizes):
        width = size.bit_length() - 1
        groups.append(list(range(low, low + width)))
        low += width
    core_bits, rest = groups[0], groups[1:]
    order = list(core_bits)
    depth = 0
    while any(depth < len(group) for group in rest):
        for group in rest:
            if depth < len(group):
                order.append(group[depth])
        depth += 1
    return order, low


def core_orders(near):
    swapped = list(near)
    swapped[1], swapped[2] = near[2], near[1]
    return (list(near), swapped)


def exchange(values, bits, count):
    pairs = [(i, i ^ (1 << bits[i & 1])) for i in range(count)]
    return lax.ppermute(values, ALL_AXES, pairs)


def scatter_sum(projected, mode_block, sizes, own):
    order, nbits = bit_order(sizes)
    count = 1 << nbits
    me = lax.axis_index(ALL_AXES)
    first_core = (me & 1) == 0
    data = projected.reshape((2,) * nbits + (mode_block, projected.shape[1]))
    near = order[: nbits - FAR_COUNT]
    orders = core_orders(near)
    presents = [list(range(nbits - 1, -1, -1)) for _ in orders]
    for step in range(len(near)):
        bits = [variant[step] for variant in orders]
        kept, sent = [], []
        for bit, present in zip(bits, presents):
            dim = present.index(bit)
            mine = (me >> bit) & 1
            kept.append(lax.dynamic_index_in_dim(data, mine, axis=dim, keepdims=False))
            sent.append(lax.dynamic_index_in_dim(data, 1 - mine, axis=dim, keepdims=False))
            present.pop(dim)
        keep = kept[0] if bits[0] == bits[1] else jnp.where(first_core, kept[0], kept[1])
        send = sent[0] if bits[0] == bits[1] else jnp.where(first_core, sent[0], sent[1])
        data = keep + exchange(send, bits, count)
    present = presents[0]
    group = tuple(f"b{bit}" for bit in present)
    data = data.reshape((1 << len(present), mode_block, projected.shape[1]))
    to_self = jnp.arange(1 << len(present))[:, None, None] == lax.axis_index(group)
    data = data + jnp.where(to_self, own[None], jnp.float32(0.0))
    data = lax.all_to_all(data, group, 0, 0, tiled=False)
    return jnp.sum(data, axis=0)


def gather_all(block, sizes):
    order, nbits = bit_order(sizes)
    count = 1 << nbits
    me = lax.axis_index(ALL_AXES)
    first_core = (me & 1) == 0
    near, far = order[: nbits - FAR_COUNT], order[nbits - FAR_COUNT :]
    orders = [list(reversed(variant)) for variant in core_orders(near)]
    presents = [sorted(far, reverse=True) for _ in orders]
    group = tuple(f"b{bit}" for bit in presents[0])
    data = jnp.broadcast_to(block[None], (1 << len(presents[0]),) + block.shape)
    data = lax.all_to_all(data, group, 0, 0, tiled=False)
    data = data.reshape((2,) * len(presents[0]) + block.shape)
    for step in range(len(near)):
        bits = [variant[step] for variant in orders]
        other = exchange(data, bits, count)
        stacked = []
        for bit, present in zip(bits, presents):
            mine = (me >> bit) & 1
            low = jnp.where(mine == 0, data, other)
            high = jnp.where(mine == 0, other, data)
            dim = sum(1 for b in present if b > bit)
            stacked.append(jnp.stack([low, high], axis=dim))
            present.insert(dim, bit)
        data = stacked[0] if bits[0] == bits[1] else jnp.where(first_core, stacked[0], stacked[1])
    return data.reshape(count * block.shape[0], block.shape[1])


def shards(coeffs, basis, observed, lift_w, lift_b, w_one, b_one, w_two, b_two, read_w):
    tile_rows, tile_cols, mode_count = basis.shape
    batch_size = coeffs.shape[1]
    sizes = (4, 8, 8, 2)
    flat_basis = basis.reshape(tile_rows * tile_cols, mode_count)
    logperm = jnp.dot(
        flat_basis,
        gather_all(coeffs, sizes),
        precision=lax.Precision.HIGHEST,
        preferred_element_type=jnp.float32,
    )
    logperm = logperm.reshape(tile_rows, tile_cols, batch_size)
    pressure, grad_field = surrogate(
        logperm, observed, lift_w, lift_b, w_one, b_one, w_two, b_two, read_w
    )
    grad_flat = grad_field.reshape(tile_rows * tile_cols, batch_size)
    projected = lax.dot_general(
        flat_basis,
        grad_flat,
        (((0,), (0,)), ((), ())),
        precision=lax.Precision.HIGHEST,
        preferred_element_type=jnp.float32,
    )
    projected = with_layout_constraint(projected, Layout(major_to_minor=(0, 1)))
    grad_coeffs = scatter_sum(projected, coeffs.shape[0], sizes, prior_weight * coeffs)
    return (pressure, grad_coeffs)


def solution(mesh):
    row_size, col_size = mesh.devices.shape
    fine = Mesh(mesh.devices.reshape((2,) * len(ALL_AXES)), ALL_AXES)
    return jax.shard_map(
        shards,
        mesh=fine,
        in_specs=(
            P(ALL_AXES, None),
            P(ROW_AXES, COL_AXES, None),
            P(ROW_AXES, COL_AXES, None),
            P(),
            P(),
            P(),
            P(),
            P(),
            P(),
            P(),
        ),
        out_specs=(P(ROW_AXES, COL_AXES, None), P(ALL_AXES, None)),
        check_vma=False,
    )
```
